32 devices in a mesh: ctx: 8 (over y, x, core), head: 4 (over z).
Axes of the slice: x: 2, y: 2, z: 4, core: 2. Of those that a mesh axis runs over, the one named last changes fastest.
Arguments:
- hidden_in: bfloat16 [4096, 5376], P('ctx'), may hold values from -40 to 40
- out_grad: bfloat16 [4096, 5376], P('ctx'), may hold values from -6 to 6
- w_query: bfloat16 [5376, 4096], P('ctx', 'head'), may hold values from -0.078125 to 0.078125
- key_weight: bfloat16 [5376, 2048], P('ctx', 'head'), may hold values from -0.078125 to 0.078125
- value_weight: bfloat16 [5376, 2048], P('ctx', 'head'), may hold values from -0.078125 to 0.078125
- w_out: bfloat16 [5376, 4096], P('ctx', 'head'), may hold values from -0.09375 to 0.09375
Outputs:
- in_grad: bfloat16 [4096, 5376], P('ctx', 'head')
- grad_query: float32 [5376, 4096], P('ctx', 'head')
- grad_key: float32 [5376, 2048], P('ctx', 'head')
- grad_value: float32 [5376, 2048], P('ctx', 'head')
- grad_out_w: float32 [5376, 4096], P('ctx', 'head')
The draws below stay inside these ranges and needn't reach their ends.
All inputs are finite; a program needn't handle non-finite values.
Results may differ from the reference program's by a relative error of at most 0.02.
Values may be sent and summed in bfloat16 or wider, within the bound.
No kernel may reach another device: no remote copies, remote signals or barrier semaphores. Data moves between devices by JAX's collectives and lax.ppermute only.
A program may use at most 256 MiB of HBM per device.

```python
import jax
import jax.numpy as jnp
from jax import lax

MODEL_WIDTH = 5376
QUERY_HEADS = 32
KEY_VALUE_HEADS = 16
HEAD_WIDTH = 128
WINDOW = 1024
S_DEV = 512
TOKENS = 4096
N_CTX = 8
N_HEAD = 4


def draw_hidden_in(key, part):
    first_key = jax.random.fold_in(jax.random.fold_in(key, 11), 0)
    base = jax.random.normal(first_key, (TOKENS, MODEL_WIDTH), jnp.float32)
    value_rows = base
    return jnp.clip(value_rows, -40.0, 40.0).astype(jnp.bfloat16)


def level_of(stream_key, extent, cuts, low, top_value):
    loudness, own = 1.0, jax.random.fold_in(stream_key, 6)
    for dim, shards_of in cuts:
        steps = jnp.exp(jax.random.uniform(jax.random.fold_in(own, dim), (shards_of,), jnp.float32, low / len(cuts), top_value / len(cuts)))
        loudness = loudness * jnp.repeat(steps, extent[dim] // shards_of).reshape([-1 if axis == dim else 1 for axis in range(len(extent))])
    return loudness


def noise(stream_key, shape, spread, most, shards=(), kind=jnp.bfloat16):
    drawn = jax.random.normal(stream_key, shape, jnp.float32) * spread
    if len(shards) > 0:
        drawn = level_of(stream_key, shape, shards, -0.22, 0.18) * drawn
    return jnp.clip(drawn, min=-most, max=most).astype(kind)


def setup_inputs(seed: int = 0) -> dict:
    seeds = jax.random.split(jax.random.key(seed), 7)
    hidden_in = draw_hidden_in(jax.random.fold_in(seeds[6], 71), 0)
    out_grad = noise(seeds[1], (TOKENS, MODEL_WIDTH), 1.0, 6.0, ((0, 8),))
    w_query = noise(seeds[2], (MODEL_WIDTH, QUERY_HEADS * HEAD_WIDTH), MODEL_WIDTH ** -0.5, 0.078125, ((0, 8), (1, 4)))
    key_weight = noise(seeds[3], (MODEL_WIDTH, KEY_VALUE_HEADS * HEAD_WIDTH), MODEL_WIDTH ** -0.5, 0.078125, ((0, 8), (1, 4)))
    value_weight = noise(seeds[4], (MODEL_WIDTH, KEY_VALUE_HEADS * HEAD_WIDTH), MODEL_WIDTH ** -0.5, 0.078125, ((0, 8), (1, 4)))
    w_out = noise(seeds[5], (MODEL_WIDTH, QUERY_HEADS * HEAD_WIDTH), (QUERY_HEADS * HEAD_WIDTH) ** -0.5, 0.09375, ((0, 8), (1, 4)))
    return dict(hidden_in=hidden_in, out_grad=out_grad, w_query=w_query, key_weight=key_weight, value_weight=value_weight, w_out=w_out)


QUERY_SCALE = 168.0 ** -0.5
ROPE_BASE = 10000.0
NEG_LARGE = -1.0e30


def rope_tables(first, count, head_size):
    half = head_size // 2
    freq = ROPE_BASE ** (-(jnp.arange(half, dtype=jnp.float32) * 2.0 / head_size))
    places = first + jnp.arange(count, dtype=jnp.int32)
    angle = places.astype(jnp.float32)[:, None] * freq[None, :]
    return jnp.cos(angle)[:, None, :], jnp.sin(angle)[:, None, :]


def apply_rotary(value_rows, cosine_table, sine_table):
    half = value_rows.shape[-1] // 2
    upper = value_rows[..., :half]
    lower = value_rows[..., half:]
    return jnp.concatenate([upper * cosine_table - lower * sine_table, lower * cosine_table + upper * sine_table], axis=-1)


def inverse_rotary(value_rows, cosine_table, sine_table):
    half = value_rows.shape[-1] // 2
    upper = value_rows[..., :half]
    lower = value_rows[..., half:]
    return jnp.concatenate([upper * cosine_table + lower * sine_table, lower * cosine_table - upper * sine_table], axis=-1)


def attend_forward(query_rows, key_rows, value_rows, allowed):
    score = jnp.einsum("ngrd,mgd->grnm", query_rows.astype(jnp.float32), key_rows.astype(jnp.float32))
    score = jnp.where(allowed[None, None], score, NEG_LARGE)
    top = jnp.max(score, axis=-1, keepdims=True)
    expo = jnp.exp(score - top)
    prob = expo / jnp.sum(expo, axis=-1, keepdims=True)
    prob_b = prob.astype(jnp.bfloat16)
    attended = jnp.einsum("grnm,mgd->ngrd", prob_b.astype(jnp.float32), value_rows.astype(jnp.float32)).astype(jnp.bfloat16)
    return prob, prob_b, attended


def attend_backward(prob, prob_b, attended, gradient_list, query_rows, key_rows, value_rows):
    delta = jnp.sum(gradient_list.astype(jnp.float32) * attended.astype(jnp.float32), axis=-1)
    delta = jnp.transpose(delta, (1, 2, 0))[..., None]
    grad_prob = jnp.einsum("ngrd,mgd->grnm", gradient_list.astype(jnp.float32), value_rows.astype(jnp.float32))
    grad_score = (prob * (grad_prob - delta)).astype(jnp.bfloat16).astype(jnp.float32)
    grad_q = jnp.einsum("grnm,mgd->ngrd", grad_score, key_rows.astype(jnp.float32))
    grad_k = jnp.einsum("grnm,ngrd->mgd", grad_score, query_rows.astype(jnp.float32))
    grad_v = jnp.einsum("grnm,ngrd->mgd", prob_b.astype(jnp.float32), gradient_list.astype(jnp.float32))
    return grad_q, grad_k, grad_v


def block_sums(left, right):
    total = jnp.zeros((left.shape[1], right.shape[1]), jnp.float32)
    for block in range(N_CTX):
        left_rows = left[block * S_DEV:(block + 1) * S_DEV]
        right_rows = right[block * S_DEV:(block + 1) * S_DEV]
        part = jnp.dot(left_rows.T, right_rows, preferred_element_type=jnp.float32)
        total = total + lax.optimization_barrier(part.astype(jnp.bfloat16)).astype(jnp.float32)
    return total


def reference(hidden_in, out_grad, w_query, key_weight, value_weight, w_out):
    token_rows = hidden_in.shape[0]
    rows = S_DEV
    reach = WINDOW // rows
    group_ratio = QUERY_HEADS // KEY_VALUE_HEADS
    span = (reach + 1) * rows
    padding_rows = reach * rows
    query = jnp.dot(hidden_in, w_query, preferred_element_type=jnp.float32)
    key_projected = jnp.dot(hidden_in, key_weight, preferred_element_type=jnp.float32)
    value_projected = jnp.dot(hidden_in, value_weight, preferred_element_type=jnp.float32)
    attention_gradient = jnp.dot(out_grad, w_out, preferred_element_type=jnp.float32).astype(jnp.bfloat16)
    cosine_table, sine_table = rope_tables(0, token_rows, HEAD_WIDTH)
    query_rows = (apply_rotary(query.reshape(token_rows, QUERY_HEADS, HEAD_WIDTH), cosine_table, sine_table) * QUERY_SCALE).astype(jnp.bfloat16)
    query_rows = query_rows.reshape(token_rows, KEY_VALUE_HEADS, group_ratio, HEAD_WIDTH)
    key_rows = apply_rotary(key_projected.reshape(token_rows, KEY_VALUE_HEADS, HEAD_WIDTH), cosine_table, sine_table).astype(jnp.bfloat16)
    value_rows = value_projected.astype(jnp.bfloat16).reshape(token_rows, KEY_VALUE_HEADS, HEAD_WIDTH)
    gradient_list = attention_gradient.reshape(token_rows, KEY_VALUE_HEADS, group_ratio, HEAD_WIDTH)
    padded_keys = jnp.concatenate([jnp.zeros((padding_rows, KEY_VALUE_HEADS, HEAD_WIDTH), jnp.bfloat16), key_rows], axis=0)
    padded_values = jnp.concatenate([jnp.zeros((padding_rows, KEY_VALUE_HEADS, HEAD_WIDTH), jnp.bfloat16), value_rows], axis=0)

    def block(carry, index):
        key_grad_total, value_grad_total = carry
        start = (index * rows).astype(jnp.int32)
        q_rows = lax.dynamic_slice_in_dim(query_rows, start, rows, 0)
        g_rows = lax.dynamic_slice_in_dim(gradient_list, start, rows, 0)
        k_rows = lax.dynamic_slice_in_dim(padded_keys, start, span, 0)
        v_rows = lax.dynamic_slice_in_dim(padded_values, start, span, 0)
        query_pos = start + jnp.arange(rows, dtype=jnp.int32)
        key_pos = start - padding_rows + jnp.arange(span, dtype=jnp.int32)
        allowed = (key_pos[None, :] <= query_pos[:, None]) & (key_pos[None, :] > query_pos[:, None] - WINDOW) & (key_pos[None, :] >= 0)
        prob, prob_b, attended = attend_forward(q_rows, k_rows, v_rows, allowed)
        grad_q, grad_k, grad_v = attend_backward(prob, prob_b, attended, g_rows, q_rows, k_rows, v_rows)
        key_grad_total = lax.dynamic_update_slice_in_dim(key_grad_total, lax.dynamic_slice_in_dim(key_grad_total, start, span, 0) + grad_k, start, 0)
        value_grad_total = lax.dynamic_update_slice_in_dim(value_grad_total, lax.dynamic_slice_in_dim(value_grad_total, start, span, 0) + grad_v, start, 0)
        return (key_grad_total, value_grad_total), (attended, grad_q)

    initial_totals = (jnp.zeros((token_rows + padding_rows, KEY_VALUE_HEADS, HEAD_WIDTH), jnp.float32), jnp.zeros((token_rows + padding_rows, KEY_VALUE_HEADS, HEAD_WIDTH), jnp.float32))
    (key_grad_total, value_grad_total), (attended, grad_q) = lax.scan(block, initial_totals, jnp.arange(N_CTX, dtype=jnp.int32))
    attended = attended.reshape(token_rows, QUERY_HEADS * HEAD_WIDTH)
    grad_q = grad_q.reshape(token_rows, QUERY_HEADS, HEAD_WIDTH)
    dquery = (inverse_rotary(grad_q, cosine_table, sine_table) * QUERY_SCALE).astype(jnp.bfloat16).reshape(token_rows, QUERY_HEADS * HEAD_WIDTH)
    key_gradient = inverse_rotary(key_grad_total[padding_rows:], cosine_table, sine_table).astype(jnp.bfloat16).reshape(token_rows, KEY_VALUE_HEADS * HEAD_WIDTH)
    value_gradient = value_grad_total[padding_rows:].astype(jnp.bfloat16).reshape(token_rows, KEY_VALUE_HEADS * HEAD_WIDTH)
    query_cols = QUERY_HEADS * HEAD_WIDTH // N_HEAD
    key_value_columns = KEY_VALUE_HEADS * HEAD_WIDTH // N_HEAD
    total = jnp.zeros((token_rows, MODEL_WIDTH), jnp.float32)
    for shard in range(N_HEAD):
        q_sel = slice(shard * query_cols, (shard + 1) * query_cols)
        k_sel = slice(shard * key_value_columns, (shard + 1) * key_value_columns)
        part = jnp.dot(dquery[:, q_sel], w_query[:, q_sel].T, preferred_element_type=jnp.float32)
        part = part + jnp.dot(key_gradient[:, k_sel], key_weight[:, k_sel].T, preferred_element_type=jnp.float32)
        part = part + jnp.dot(value_gradient[:, k_sel], value_weight[:, k_sel].T, preferred_element_type=jnp.float32)
        total = total + lax.optimization_barrier(part.astype(jnp.bfloat16)).astype(jnp.float32)
    in_grad = total.astype(jnp.bfloat16)
    grad_query = block_sums(hidden_in, dquery)
    grad_key = block_sums(hidden_in, key_gradient)
    grad_value = block_sums(hidden_in, value_gradient)
    grad_out_w = block_sums(out_grad, attended)
    return (in_grad, grad_query, grad_key, grad_value, grad_out_w)
```

```python
import jax
import jax.numpy as jnp
from jax import lax
from jax.sharding import PartitionSpec as P

HEAD_WIDTH = 128
WINDOW = 1024


QUERY_SCALE = 168.0 ** (-0.5)
ROPE_BASE = 10000.0
NEG_LARGE = -1e30


def from_behind(value, axis, steps):
    count = lax.axis_size(axis)
    initial, last = (max(0, -steps), min(count, count - steps))
    return lax.ppermute(value, axis, [(source, source + steps) for source in range(initial, last)])


def rope_tables(first, count, head_size):
    half = head_size // 2
    freq = ROPE_BASE ** (-(jnp.arange(half, dtype=jnp.float32) * 2.0 / head_size))
    places = first + jnp.arange(count, dtype=jnp.int32)
    angle = places.astype(jnp.float32)[:, None] * freq[None, :]
    return (jnp.cos(angle)[:, None, :], jnp.sin(angle)[:, None, :])


def apply_rotary(value_rows, cosine_table, sine_table):
    half = value_rows.shape[-1] // 2
    upper = value_rows[..., :half]
    lower = value_rows[..., half:]
    return jnp.concatenate(
        [upper * cosine_table - lower * sine_table, lower * cosine_table + upper * sine_table],
        axis=-1,
    )


def inverse_rotary(value_rows, cosine_table, sine_table):
    half = value_rows.shape[-1] // 2
    upper = value_rows[..., :half]
    lower = value_rows[..., half:]
    return jnp.concatenate(
        [upper * cosine_table + lower * sine_table, lower * cosine_table - upper * sine_table],
        axis=-1,
    )


def dot_rows(left, weight):
    return lax.dot_general(
        left, weight, (((1,), (1,)), ((), ())), preferred_element_type=jnp.float32
    )


def gather_rows(value):
    return lax.all_gather(value, "ctx", axis=0, tiled=True)


def block_sums(left, right, blocks):
    rows = left.shape[0] // blocks
    left = left.reshape(blocks, rows, left.shape[1])
    right = right.reshape(blocks, rows, right.shape[1])
    parts = jnp.einsum("bnd,bnc->bdc", left, right, preferred_element_type=jnp.float32)
    return jnp.sum(parts.astype(jnp.bfloat16).astype(jnp.float32), axis=0)

def attend_forward(query_rows, key_rows, value_rows, allowed):
    score = jnp.einsum("ngrd,mgd->grnm", query_rows, key_rows, preferred_element_type=jnp.float32)
    score = jnp.where(allowed[None, None], score, NEG_LARGE)
    top = jnp.max(score, axis=-1, keepdims=True)
    expo = jnp.exp(score - top)
    prob = expo / jnp.sum(expo, axis=-1, keepdims=True)
    prob_b = prob.astype(jnp.bfloat16)
    attended = jnp.einsum(
        "grnm,mgd->ngrd", prob_b, value_rows, preferred_element_type=jnp.float32
    ).astype(jnp.bfloat16)
    return (prob, prob_b, attended)


def attend_backward(prob, prob_b, attended, gradient_list, query_rows, key_rows, value_rows):
    delta = jnp.sum(gradient_list.astype(jnp.float32) * attended.astype(jnp.float32), axis=-1)
    delta = jnp.transpose(delta, (1, 2, 0))[..., None]
    grad_prob = jnp.einsum(
        "ngrd,mgd->grnm", gradient_list, value_rows, preferred_element_type=jnp.float32
    )
    grad_score = (prob * (grad_prob - delta)).astype(jnp.bfloat16)
    grad_q = jnp.einsum("grnm,mgd->ngrd", grad_score, key_rows, preferred_element_type=jnp.float32)
    grad_k = jnp.einsum(
        "grnm,ngrd->mgd", grad_score, query_rows, preferred_element_type=jnp.float32
    )
    grad_v = jnp.einsum("grnm,ngrd->mgd", prob_b, gradient_list, preferred_element_type=jnp.float32)
    return (grad_q, grad_k, grad_v)


def shards(hidden_in, out_grad, w_query, key_weight, value_weight, w_out):
    rows = hidden_in.shape[0]
    head_size = HEAD_WIDTH
    query_cols = w_query.shape[1]
    key_value_columns = key_weight.shape[1]
    local_heads = query_cols // head_size
    local_groups = key_value_columns // head_size
    group_ratio = local_heads // local_groups
    reach = WINDOW // rows
    first = lax.axis_index("ctx") * rows
    full_query, full_key, full_value, full_out = (
        lax.all_gather(w_query, "ctx", axis=0, tiled=True),
        lax.all_gather(key_weight, "ctx", axis=0, tiled=True),
        lax.all_gather(value_weight, "ctx", axis=0, tiled=True),
        lax.all_gather(w_out, "ctx", axis=0, tiled=True),
    )
    query = jnp.dot(hidden_in, full_query, preferred_element_type=jnp.float32)
    key_projected = jnp.dot(hidden_in, full_key, preferred_element_type=jnp.float32)
    value_projected = jnp.dot(hidden_in, full_value, preferred_element_type=jnp.float32)
    grad_att_f = jnp.dot(out_grad, full_out, preferred_element_type=jnp.float32)
    cosine_table, sine_table = rope_tables(first, rows, head_size)
    query_rows = (
        apply_rotary(query.reshape(rows, local_heads, head_size), cosine_table, sine_table)
        * QUERY_SCALE
    ).astype(jnp.bfloat16)
    keys_here = (
        apply_rotary(key_projected.reshape(rows, local_groups, head_size), cosine_table, sine_table)
        .astype(jnp.bfloat16)
        .reshape(rows, key_value_columns)
    )
    values_here = value_projected.astype(jnp.bfloat16)
    attention_gradient = grad_att_f.astype(jnp.bfloat16)
    key_blocks = []
    value_blocks = []
    for distance in range(reach, 0, -1):
        far_keys, far_values = from_behind((keys_here, values_here), "ctx", distance)
        key_blocks.append(far_keys)
        value_blocks.append(far_values)
    keys_all = jnp.concatenate(key_blocks + [keys_here], axis=0).reshape(
        -1, local_groups, head_size
    )
    values_all = jnp.concatenate(value_blocks + [values_here], axis=0).reshape(
        -1, local_groups, head_size
    )
    query_pos = first + jnp.arange(rows, dtype=jnp.int32)
    key_pos = first - reach * rows + jnp.arange((reach + 1) * rows, dtype=jnp.int32)
    allowed = (
        (key_pos[None, :] <= query_pos[:, None])
        & (key_pos[None, :] > query_pos[:, None] - WINDOW)
        & (key_pos[None, :] >= 0)
    )
    grouped_queries = query_rows.reshape(rows, local_groups, group_ratio, head_size)
    grouped_grads = attention_gradient.reshape(rows, local_groups, group_ratio, head_size)
    prob, prob_b, attended = attend_forward(grouped_queries, keys_all, values_all, allowed)
    attended_flat = attended.reshape(rows, query_cols)
    grad_q, grad_k, grad_v = attend_backward(
        prob, prob_b, attended, grouped_grads, grouped_queries, keys_all, values_all
    )
    grad_k = grad_k.reshape(-1, key_value_columns)
    grad_v = grad_v.reshape(-1, key_value_columns)
    own_keys = grad_k[reach * rows :]
    own_values = grad_v[reach * rows :]
    for distance in range(1, reach + 1):
        lowest = (reach - distance) * rows
        back_keys, back_values = from_behind(
            (grad_k[lowest : lowest + rows], grad_v[lowest : lowest + rows]), "ctx", -distance
        )
        own_keys = own_keys + back_keys
        own_values = own_values + back_values
    dquery = (
        (
            inverse_rotary(grad_q.reshape(rows, local_heads, head_size), cosine_table, sine_table)
            * QUERY_SCALE
        )
        .astype(jnp.bfloat16)
        .reshape(rows, query_cols)
    )
    key_gradient = (
        inverse_rotary(own_keys.reshape(rows, local_groups, head_size), cosine_table, sine_table)
        .astype(jnp.bfloat16)
        .reshape(rows, key_value_columns)
    )
    value_gradient = own_values.astype(jnp.bfloat16)
    partial_in = (
        dot_rows(dquery, full_query)
        + dot_rows(key_gradient, full_key)
        + dot_rows(value_gradient, full_value)
    )
    in_grad = lax.psum_scatter(
        partial_in.astype(jnp.bfloat16), "head", scatter_dimension=1, tiled=True
    )
    n_ctx = lax.axis_size("ctx")
    hidden_cols = lax.all_to_all(hidden_in, "ctx", 1, 0, tiled=True)
    out_grad_cols = lax.all_to_all(out_grad, "ctx", 1, 0, tiled=True)
    grad_query = block_sums(hidden_cols, gather_rows(dquery), n_ctx)
    grad_key = block_sums(hidden_cols, gather_rows(key_gradient), n_ctx)
    grad_value = block_sums(hidden_cols, gather_rows(value_gradient), n_ctx)
    grad_out_w = block_sums(out_grad_cols, gather_rows(attended_flat), n_ctx)
    return (in_grad, grad_query, grad_key, grad_value, grad_out_w)


def solution(mesh):
    in_specs = (
        P("ctx", None),
        P("ctx", None),
        P("ctx", "head"),
        P("ctx", "head"),
        P("ctx", "head"),
        P("ctx", "head"),
    )
    out_specs = (
        P("ctx", "head"),
        P("ctx", "head"),
        P("ctx", "head"),
        P("ctx", "head"),
        P("ctx", "head"),
    )
    return jax.shard_map(shards, mesh=mesh, in_specs=in_specs, out_specs=out_specs, check_vma=False)
```

```python
import jax
import jax.numpy as jnp
from jax import lax
from jax.sharding import PartitionSpec as P
from jax.experimental.layout import Layout, with_layout_constraint

HEAD_WIDTH = 128
WINDOW = 1024


QUERY_SCALE = 168.0 ** (-0.5)
ROPE_BASE = 10000.0
NEG_LARGE = -1e30


def from_behind(value, axis, steps):
    count = lax.axis_size(axis)
    initial, last = (max(0, -steps), min(count, count - steps))
    return lax.ppermute(value, axis, [(source, source + steps) for source in range(initial, last)])


def rope_tables(first, count, head_size):
    half = head_size // 2
    freq = ROPE_BASE ** (-(jnp.arange(half, dtype=jnp.float32) * 2.0 / head_size))
    places = first + jnp.arange(count, dtype=jnp.int32)
    angle = places.astype(jnp.float32)[:, None] * freq[None, :]
    return (jnp.cos(angle)[:, None, :], jnp.sin(angle)[:, None, :])


def apply_rotary(value_rows, cosine_table, sine_table):
    half = value_rows.shape[-1] // 2
    upper = value_rows[..., :half]
    lower = value_rows[..., half:]
    return jnp.concatenate(
        [upper * cosine_table - lower * sine_table, lower * cosine_table + upper * sine_table],
        axis=-1,
    )


def inverse_rotary(value_rows, cosine_table, sine_table):
    half = value_rows.shape[-1] // 2
    upper = value_rows[..., :half]
    lower = value_rows[..., half:]
    return jnp.concatenate(
        [upper * cosine_table + lower * sine_table, lower * cosine_table - upper * sine_table],
        axis=-1,
    )


def dot_rows(left, weight):
    return lax.dot_general(
        left, weight, (((1,), (1,)), ((), ())), preferred_element_type=jnp.float32
    )


def gather_rows(value):
    value = with_layout_constraint(value, Layout((0, 1)))
    gathered = lax.all_gather(value, "ctx", axis=0, tiled=False)
    return with_layout_constraint(gathered, Layout((0, 1, 2)))


def columns_of(value, blocks):
    rows, width = value.shape
    split = jnp.transpose(value.reshape(rows, blocks, width // blocks), (1, 0, 2))
    return lax.all_to_all(split, "ctx", 0, 0, tiled=False)


def block_sums(left, right):
    parts = jnp.einsum("bnd,bnc->bdc", left, right, preferred_element_type=jnp.float32)
    return jnp.sum(parts.astype(jnp.bfloat16).astype(jnp.float32), axis=0)

def attend_forward(query_rows, key_rows, value_rows, allowed):
    score = jnp.einsum("ngrd,mgd->grnm", query_rows, key_rows, preferred_element_type=jnp.float32)
    score = jnp.where(allowed[None, None], score, NEG_LARGE)
    top = jnp.max(score, axis=-1, keepdims=True)
    expo = jnp.exp(score - top)
    prob = expo / jnp.sum(expo, axis=-1, keepdims=True)
    prob_b = prob.astype(jnp.bfloat16)
    attended = jnp.einsum(
        "grnm,mgd->ngrd", prob_b, value_rows, preferred_element_type=jnp.float32
    ).astype(jnp.bfloat16)
    return (prob, prob_b, attended)


def attend_backward(prob, prob_b, attended, gradient_list, query_rows, key_rows, value_rows):
    delta = jnp.sum(gradient_list.astype(jnp.float32) * attended.astype(jnp.float32), axis=-1)
    delta = jnp.transpose(delta, (1, 2, 0))[..., None]
    grad_prob = jnp.einsum(
        "ngrd,mgd->grnm", gradient_list, value_rows, preferred_element_type=jnp.float32
    )
    grad_score = (prob * (grad_prob - delta)).astype(jnp.bfloat16)
    grad_q = jnp.einsum("grnm,mgd->ngrd", grad_score, key_rows, preferred_element_type=jnp.float32)
    grad_k = jnp.einsum(
        "grnm,ngrd->mgd", grad_score, query_rows, preferred_element_type=jnp.float32
    )
    grad_v = jnp.einsum("grnm,ngrd->mgd", prob_b, gradient_list, preferred_element_type=jnp.float32)
    return (grad_q, grad_k, grad_v)


def shards(hidden_in, out_grad, w_query, key_weight, value_weight, w_out):
    rows = hidden_in.shape[0]
    head_size = HEAD_WIDTH
    query_cols = w_query.shape[1]
    key_value_columns = key_weight.shape[1]
    local_heads = query_cols // head_size
    local_groups = key_value_columns // head_size
    group_ratio = local_heads // local_groups
    reach = WINDOW // rows
    first = lax.axis_index("ctx") * rows
    full_query, full_key, full_value, full_out = (
        lax.all_gather(w_query, "ctx", axis=0, tiled=True),
        lax.all_gather(key_weight, "ctx", axis=0, tiled=True),
        lax.all_gather(value_weight, "ctx", axis=0, tiled=True),
        lax.all_gather(w_out, "ctx", axis=0, tiled=True),
    )
    query = jnp.dot(hidden_in, full_query, preferred_element_type=jnp.float32)
    key_projected = jnp.dot(hidden_in, full_key, preferred_element_type=jnp.float32)
    value_projected = jnp.dot(hidden_in, full_value, preferred_element_type=jnp.float32)
    grad_att_f = jnp.dot(out_grad, full_out, preferred_element_type=jnp.float32)
    cosine_table, sine_table = rope_tables(first, rows, head_size)
    query_rows = (
        apply_rotary(query.reshape(rows, local_heads, head_size), cosine_table, sine_table)
        * QUERY_SCALE
    ).astype(jnp.bfloat16)
    keys_here = (
        apply_rotary(key_projected.reshape(rows, local_groups, head_size), cosine_table, sine_table)
        .astype(jnp.bfloat16)
        .reshape(rows, key_value_columns)
    )
    values_here = value_projected.astype(jnp.bfloat16)
    attention_gradient = grad_att_f.astype(jnp.bfloat16)
    key_blocks = []
    value_blocks = []
    for distance in range(reach, 0, -1):
        far_keys, far_values = from_behind((keys_here, values_here), "ctx", distance)
        key_blocks.append(far_keys)
        value_blocks.append(far_values)
    keys_all = jnp.concatenate(key_blocks + [keys_here], axis=0).reshape(
        -1, local_groups, head_size
    )
    values_all = jnp.concatenate(value_blocks + [values_here], axis=0).reshape(
        -1, local_groups, head_size
    )
    query_pos = first + jnp.arange(rows, dtype=jnp.int32)
    key_pos = first - reach * rows + jnp.arange((reach + 1) * rows, dtype=jnp.int32)
    allowed = (
        (key_pos[None, :] <= query_pos[:, None])
        & (key_pos[None, :] > query_pos[:, None] - WINDOW)
        & (key_pos[None, :] >= 0)
    )
    grouped_queries = query_rows.reshape(rows, local_groups, group_ratio, head_size)
    grouped_grads = attention_gradient.reshape(rows, local_groups, group_ratio, head_size)
    prob, prob_b, attended = attend_forward(grouped_queries, keys_all, values_all, allowed)
    attended_flat = attended.reshape(rows, query_cols)
    grad_q, grad_k, grad_v = attend_backward(
        prob, prob_b, attended, grouped_grads, grouped_queries, keys_all, values_all
    )
    grad_k = grad_k.reshape(-1, key_value_columns)
    grad_v = grad_v.reshape(-1, key_value_columns)
    own_keys = grad_k[reach * rows :]
    own_values = grad_v[reach * rows :]
    for distance in range(1, reach + 1):
        lowest = (reach - distance) * rows
        back_keys, back_values = from_behind(
            (grad_k[lowest : lowest + rows], grad_v[lowest : lowest + rows]), "ctx", -distance
        )
        own_keys = own_keys + back_keys
        own_values = own_values + back_values
    dquery = (
        (
            inverse_rotary(grad_q.reshape(rows, local_heads, head_size), cosine_table, sine_table)
            * QUERY_SCALE
        )
        .astype(jnp.bfloat16)
        .reshape(rows, query_cols)
    )
    key_gradient = (
        inverse_rotary(own_keys.reshape(rows, local_groups, head_size), cosine_table, sine_table)
        .astype(jnp.bfloat16)
        .reshape(rows, key_value_columns)
    )
    value_gradient = own_values.astype(jnp.bfloat16)
    partial_in = (
        dot_rows(dquery, full_query)
        + dot_rows(key_gradient, full_key)
        + dot_rows(value_gradient, full_value)
    )
    in_grad = lax.psum_scatter(
        partial_in.astype(jnp.bfloat16), "head", scatter_dimension=1, tiled=True
    )
    n_ctx = lax.axis_size("ctx")
    hidden_cols = columns_of(hidden_in, n_ctx)
    out_grad_cols = columns_of(out_grad, n_ctx)
    grad_query = block_sums(hidden_cols, gather_rows(dquery))
    key_value_sums = block_sums(
        hidden_cols, gather_rows(jnp.concatenate([key_gradient, value_gradient], axis=1))
    )
    grad_key = key_value_sums[:, :key_value_columns]
    grad_value = key_value_sums[:, key_value_columns:]
    grad_out_w = block_sums(out_grad_cols, gather_rows(attended_flat))
    return (in_grad, grad_query, grad_key, grad_value, grad_out_w)


def solution(mesh):
    in_specs = (
        P("ctx", None),
        P("ctx", None),
        P("ctx", "head"),
        P("ctx", "head"),
        P("ctx", "head"),
        P("ctx", "head"),
    )
    out_specs = (
        P("ctx", "head"),
        P("ctx", "head"),
        P("ctx", "head"),
        P("ctx", "head"),
        P("ctx", "head"),
    )
    return jax.shard_map(shards, mesh=mesh, in_specs=in_specs, out_specs=out_specs, check_vma=False)
```

```python
import jax
import jax.numpy as jnp
from jax import lax
from jax.sharding import Mesh, PartitionSpec as P

HEAD_WIDTH = 128
WINDOW = 1024


QUERY_SCALE = 168.0 ** (-0.5)
ROPE_BASE = 10000.0
NEG_LARGE = -1e30


CTX = ("chip", "core")


def from_behind(value, axis, steps):
    count = lax.axis_size(axis)
    initial, last = (max(0, -steps), min(count, count - steps))
    return lax.ppermute(value, axis, [(source, source + steps) for source in range(initial, last)])


def rope_tables(first, count, head_size):
    half = head_size // 2
    freq = ROPE_BASE ** (-(jnp.arange(half, dtype=jnp.float32) * 2.0 / head_size))
    places = first + jnp.arange(count, dtype=jnp.int32)
    angle = places.astype(jnp.float32)[:, None] * freq[None, :]
    return (jnp.cos(angle)[:, None, :], jnp.sin(angle)[:, None, :])


def apply_rotary(value_rows, cosine_table, sine_table):
    half = value_rows.shape[-1] // 2
    upper = value_rows[..., :half]
    lower = value_rows[..., half:]
    return jnp.concatenate(
        [upper * cosine_table - lower * sine_table, lower * cosine_table + upper * sine_table],
        axis=-1,
    )


def inverse_rotary(value_rows, cosine_table, sine_table):
    half = value_rows.shape[-1] // 2
    upper = value_rows[..., :half]
    lower = value_rows[..., half:]
    return jnp.concatenate(
        [upper * cosine_table + lower * sine_table, lower * cosine_table - upper * sine_table],
        axis=-1,
    )


def gather_weight(weight):
    mine = lax.all_gather(weight, "chip", axis=0, tiled=False)
    other = lax.ppermute(mine, "core", [(0, 1), (1, 0)])
    return (mine, other)


def split_columns(value, core, n_chip, width):
    blocks = value.reshape(value.shape[0], n_chip, 2, width)
    mine = lax.dynamic_index_in_dim(blocks, core, axis=2, keepdims=False)
    other = lax.dynamic_index_in_dim(blocks, 1 - core, axis=2, keepdims=False)
    return (mine, other)


def project(halves, weights):
    total = None
    for left, right in zip(halves, weights):
        part = jnp.einsum("nkd,kdc->nc", left, right, preferred_element_type=jnp.float32)
        total = part if total is None else total + part
    return total


def back_project(grads, weight):
    return jnp.einsum("nc,kdc->nkd", grads, weight, preferred_element_type=jnp.float32)

def dot_rows(left, weight):
    return lax.dot_general(
        left, weight, (((1,), (1,)), ((), ())), preferred_element_type=jnp.float32
    )


def attend_forward(query_rows, key_rows, value_rows, allowed):
    score = jnp.einsum("ngrd,mgd->grnm", query_rows, key_rows, preferred_element_type=jnp.float32)
    score = jnp.where(allowed[None, None], score, NEG_LARGE)
    top = jnp.max(score, axis=-1, keepdims=True)
    expo = jnp.exp(score - top)
    prob = expo / jnp.sum(expo, axis=-1, keepdims=True)
    prob_b = prob.astype(jnp.bfloat16)
    attended = jnp.einsum(
        "grnm,mgd->ngrd", prob_b, value_rows, preferred_element_type=jnp.float32
    ).astype(jnp.bfloat16)
    return (prob, prob_b, attended)


def attend_backward(prob, prob_b, attended, gradient_list, query_rows, key_rows, value_rows):
    delta = jnp.sum(gradient_list.astype(jnp.float32) * attended.astype(jnp.float32), axis=-1)
    delta = jnp.transpose(delta, (1, 2, 0))[..., None]
    grad_prob = jnp.einsum(
        "ngrd,mgd->grnm", gradient_list, value_rows, preferred_element_type=jnp.float32
    )
    grad_score = (prob * (grad_prob - delta)).astype(jnp.bfloat16)
    grad_q = jnp.einsum("grnm,mgd->ngrd", grad_score, key_rows, preferred_element_type=jnp.float32)
    grad_k = jnp.einsum(
        "grnm,ngrd->mgd", grad_score, query_rows, preferred_element_type=jnp.float32
    )
    grad_v = jnp.einsum("grnm,ngrd->mgd", prob_b, gradient_list, preferred_element_type=jnp.float32)
    return (grad_q, grad_k, grad_v)


def shards(hidden_in, out_grad, w_query, key_weight, value_weight, w_out):
    rows = hidden_in.shape[0]
    head_size = HEAD_WIDTH
    query_cols = w_query.shape[1]
    key_value_columns = key_weight.shape[1]
    local_heads = query_cols // head_size
    local_groups = key_value_columns // head_size
    group_ratio = local_heads // local_groups
    reach = WINDOW // rows
    core = lax.axis_index("core")
    first = (lax.axis_index("chip") * lax.axis_size("core") + core) * rows
    n_chip = lax.axis_size("chip")
    weight_rows = w_query.shape[0]
    full_key = gather_weight(key_weight)
    full_value = gather_weight(value_weight)
    full_query = gather_weight(w_query)
    full_out = gather_weight(w_out)
    hidden_halves = split_columns(hidden_in, core, n_chip, weight_rows)
    out_grad_halves = split_columns(out_grad, core, n_chip, weight_rows)
    key_projected = project(hidden_halves, full_key)
    value_projected = project(hidden_halves, full_value)
    query = project(hidden_halves, full_query)
    grad_att_f = project(out_grad_halves, full_out)
    cosine_table, sine_table = rope_tables(first, rows, head_size)
    query_rows = (
        apply_rotary(query.reshape(rows, local_heads, head_size), cosine_table, sine_table)
        * QUERY_SCALE
    ).astype(jnp.bfloat16)
    keys_here = (
        apply_rotary(key_projected.reshape(rows, local_groups, head_size), cosine_table, sine_table)
        .astype(jnp.bfloat16)
        .reshape(rows, key_value_columns)
    )
    values_here = value_projected.astype(jnp.bfloat16)
    attention_gradient = grad_att_f.astype(jnp.bfloat16)
    key_blocks = []
    value_blocks = []
    for distance in range(reach, 0, -1):
        far_keys, far_values = from_behind((keys_here, values_here), CTX, distance)
        key_blocks.append(far_keys)
        value_blocks.append(far_values)
    keys_all = jnp.concatenate(key_blocks + [keys_here], axis=0).reshape(
        -1, local_groups, head_size
    )
    values_all = jnp.concatenate(value_blocks + [values_here], axis=0).reshape(
        -1, local_groups, head_size
    )
    query_pos = first + jnp.arange(rows, dtype=jnp.int32)
    key_pos = first - reach * rows + jnp.arange((reach + 1) * rows, dtype=jnp.int32)
    allowed = (
        (key_pos[None, :] <= query_pos[:, None])
        & (key_pos[None, :] > query_pos[:, None] - WINDOW)
        & (key_pos[None, :] >= 0)
    )
    grouped_queries = query_rows.reshape(rows, local_groups, group_ratio, head_size)
    grouped_grads = attention_gradient.reshape(rows, local_groups, group_ratio, head_size)
    prob, prob_b, attended = attend_forward(grouped_queries, keys_all, values_all, allowed)
    attended_flat = attended.reshape(rows, query_cols)
    grad_w_out = jnp.einsum(
        "nd,nc->dc", out_grad, attended_flat, preferred_element_type=jnp.float32
    )
    grad_q, grad_k, grad_v = attend_backward(
        prob, prob_b, attended, grouped_grads, grouped_queries, keys_all, values_all
    )
    grad_k = grad_k.reshape(-1, key_value_columns)
    grad_v = grad_v.reshape(-1, key_value_columns)
    own_keys = grad_k[reach * rows :]
    own_values = grad_v[reach * rows :]
    for distance in range(1, reach + 1):
        lowest = (reach - distance) * rows
        back_keys, back_values = from_behind(
            (grad_k[lowest : lowest + rows], grad_v[lowest : lowest + rows]), CTX, -distance
        )
        own_keys = own_keys + back_keys
        own_values = own_values + back_values
    dquery = (
        (
            inverse_rotary(grad_q.reshape(rows, local_heads, head_size), cosine_table, sine_table)
            * QUERY_SCALE
        )
        .astype(jnp.bfloat16)
        .reshape(rows, query_cols)
    )
    key_gradient = (
        inverse_rotary(own_keys.reshape(rows, local_groups, head_size), cosine_table, sine_table)
        .astype(jnp.bfloat16)
        .reshape(rows, key_value_columns)
    )
    value_gradient = own_values.astype(jnp.bfloat16)
    halves = [
        back_project(dquery, full_query[side])
        + back_project(key_gradient, full_key[side])
        + back_project(value_gradient, full_value[side])
        for side in range(2)
    ]
    partial_in = jnp.where(
        core == 0, jnp.stack(halves, axis=2), jnp.stack(halves[::-1], axis=2)
    ).astype(jnp.bfloat16).reshape(rows, -1)
    in_grad = lax.psum_scatter(partial_in, "head", scatter_dimension=1, tiled=True)
    grad_q_part = jnp.einsum("nd,nc->dc", hidden_in, dquery, preferred_element_type=jnp.float32)
    grad_k_part = jnp.einsum(
        "nd,nc->dc", hidden_in, key_gradient, preferred_element_type=jnp.float32
    )
    grad_v_part = jnp.einsum(
        "nd,nc->dc", hidden_in, value_gradient, preferred_element_type=jnp.float32
    )
    grad_query, grad_key, grad_value, grad_out_w = (
        lax.psum_scatter(
            grad_q_part.astype(jnp.bfloat16), CTX, scatter_dimension=0, tiled=True
        ).astype(jnp.float32),
        lax.psum_scatter(
            grad_k_part.astype(jnp.bfloat16), CTX, scatter_dimension=0, tiled=True
        ).astype(jnp.float32),
        lax.psum_scatter(
            grad_v_part.astype(jnp.bfloat16), CTX, scatter_dimension=0, tiled=True
        ).astype(jnp.float32),
        lax.psum_scatter(
            grad_w_out.astype(jnp.bfloat16), CTX, scatter_dimension=0, tiled=True
        ).astype(jnp.float32),
    )
    return (in_grad, grad_query, grad_key, grad_value, grad_out_w)


def solution(mesh):
    n_ctx, n_head = mesh.shape["ctx"], mesh.shape["head"]
    split = Mesh(mesh.devices.reshape(n_ctx // 2, 2, n_head), ("chip", "core", "head"))
    in_specs = (P(CTX, None), P(CTX, None)) + (P(CTX, "head"),) * 4
    out_specs = (P(CTX, "head"),) * 5
    return jax.shard_map(shards, mesh=split, in_specs=in_specs, out_specs=out_specs, check_vma=False)
```

```python
import jax
import jax.numpy as jnp
from jax import lax
from jax.sharding import PartitionSpec as P

HEAD_WIDTH = 128
WINDOW = 1024


QUERY_SCALE = 168.0 ** (-0.5)
ROPE_BASE = 10000.0
NEG_LARGE = -1e30


def from_behind(value, axis, steps):
    count = lax.axis_size(axis)
    initial, last = (max(0, -steps), min(count, count - steps))
    return lax.ppermute(value, axis, [(source, source + steps) for source in range(initial, last)])


def rope_tables(first, count, head_size):
    half = head_size // 2
    freq = ROPE_BASE ** (-(jnp.arange(half, dtype=jnp.float32) * 2.0 / head_size))
    places = first + jnp.arange(count, dtype=jnp.int32)
    angle = places.astype(jnp.float32)[:, None] * freq[None, :]
    return (jnp.cos(angle)[:, None, :], jnp.sin(angle)[:, None, :])


def apply_rotary(value_rows, cosine_table, sine_table):
    half = value_rows.shape[-1] // 2
    upper = value_rows[..., :half]
    lower = value_rows[..., half:]
    return jnp.concatenate(
        [upper * cosine_table - lower * sine_table, lower * cosine_table + upper * sine_table],
        axis=-1,
    )


def inverse_rotary(value_rows, cosine_table, sine_table):
    half = value_rows.shape[-1] // 2
    upper = value_rows[..., :half]
    lower = value_rows[..., half:]
    return jnp.concatenate(
        [upper * cosine_table + lower * sine_table, lower * cosine_table - upper * sine_table],
        axis=-1,
    )


def dot_rows(left, weight):
    return lax.dot_general(
        left, weight, (((1,), (1,)), ((), ())), preferred_element_type=jnp.float32
    )


def attend_forward(query_rows, key_rows, value_rows, allowed):
    score = jnp.einsum("ngrd,mgd->grnm", query_rows, key_rows, preferred_element_type=jnp.float32)
    score = jnp.where(allowed[None, None], score, NEG_LARGE)
    top = jnp.max(score, axis=-1, keepdims=True)
    expo = jnp.exp(score - top)
    prob = expo / jnp.sum(expo, axis=-1, keepdims=True)
    prob_b = prob.astype(jnp.bfloat16)
    attended = jnp.einsum(
        "grnm,mgd->ngrd", prob_b, value_rows, preferred_element_type=jnp.float32
    ).astype(jnp.bfloat16)
    return (prob, prob_b, attended)


def attend_backward(prob, prob_b, attended, gradient_list, query_rows, key_rows, value_rows):
    delta = jnp.sum(gradient_list.astype(jnp.float32) * attended.astype(jnp.float32), axis=-1)
    delta = jnp.transpose(delta, (1, 2, 0))[..., None]
    grad_prob = jnp.einsum(
        "ngrd,mgd->grnm", gradient_list, value_rows, preferred_element_type=jnp.float32
    )
    grad_score = (prob * (grad_prob - delta)).astype(jnp.bfloat16)
    grad_q = jnp.einsum("grnm,mgd->ngrd", grad_score, key_rows, preferred_element_type=jnp.float32)
    grad_k = jnp.einsum(
        "grnm,ngrd->mgd", grad_score, query_rows, preferred_element_type=jnp.float32
    )
    grad_v = jnp.einsum("grnm,ngrd->mgd", prob_b, gradient_list, preferred_element_type=jnp.float32)
    return (grad_q, grad_k, grad_v)


def shards(hidden_in, out_grad, w_query, key_weight, value_weight, w_out):
    rows = hidden_in.shape[0]
    head_size = HEAD_WIDTH
    query_cols = w_query.shape[1]
    key_value_columns = key_weight.shape[1]
    local_heads = query_cols // head_size
    local_groups = key_value_columns // head_size
    group_ratio = local_heads // local_groups
    reach = WINDOW // rows
    first = lax.axis_index("ctx") * rows
    full_qkv = lax.all_gather(
        jnp.concatenate([w_query, key_weight, value_weight], axis=1), "ctx", axis=0, tiled=True
    )
    full_out = lax.all_gather(w_out, "ctx", axis=0, tiled=True)
    projected = jnp.dot(hidden_in, full_qkv, preferred_element_type=jnp.float32)
    query = projected[:, :query_cols]
    key_projected = projected[:, query_cols : query_cols + key_value_columns]
    value_projected = projected[:, query_cols + key_value_columns :]
    grad_att_f = jnp.dot(out_grad, full_out, preferred_element_type=jnp.float32)
    cosine_table, sine_table = rope_tables(first, rows, head_size)
    query_rows = (
        apply_rotary(query.reshape(rows, local_heads, head_size), cosine_table, sine_table)
        * QUERY_SCALE
    ).astype(jnp.bfloat16)
    keys_here = (
        apply_rotary(key_projected.reshape(rows, local_groups, head_size), cosine_table, sine_table)
        .astype(jnp.bfloat16)
        .reshape(rows, key_value_columns)
    )
    values_here = value_projected.astype(jnp.bfloat16)
    attention_gradient = grad_att_f.astype(jnp.bfloat16)
    key_blocks = []
    value_blocks = []
    for distance in range(reach, 0, -1):
        far_keys, far_values = from_behind((keys_here, values_here), "ctx", distance)
        key_blocks.append(far_keys)
        value_blocks.append(far_values)
    keys_all = jnp.concatenate(key_blocks + [keys_here], axis=0).reshape(
        -1, local_groups, head_size
    )
    values_all = jnp.concatenate(value_blocks + [values_here], axis=0).reshape(
        -1, local_groups, head_size
    )
    query_pos = first + jnp.arange(rows, dtype=jnp.int32)
    key_pos = first - reach * rows + jnp.arange((reach + 1) * rows, dtype=jnp.int32)
    allowed = (
        (key_pos[None, :] <= query_pos[:, None])
        & (key_pos[None, :] > query_pos[:, None] - WINDOW)
        & (key_pos[None, :] >= 0)
    )
    grouped_queries = query_rows.reshape(rows, local_groups, group_ratio, head_size)
    grouped_grads = attention_gradient.reshape(rows, local_groups, group_ratio, head_size)
    prob, prob_b, attended = attend_forward(grouped_queries, keys_all, values_all, allowed)
    attended_flat = attended.reshape(rows, query_cols)
    grad_w_out = jnp.einsum(
        "nd,nc->dc", out_grad, attended_flat, preferred_element_type=jnp.float32
    )
    grad_q, grad_k, grad_v = attend_backward(
        prob, prob_b, attended, grouped_grads, grouped_queries, keys_all, values_all
    )
    grad_k = grad_k.reshape(-1, key_value_columns)
    grad_v = grad_v.reshape(-1, key_value_columns)
    own_keys = grad_k[reach * rows :]
    own_values = grad_v[reach * rows :]
    for distance in range(1, reach + 1):
        lowest = (reach - distance) * rows
        back_keys, back_values = from_behind(
            (grad_k[lowest : lowest + rows], grad_v[lowest : lowest + rows]), "ctx", -distance
        )
        own_keys = own_keys + back_keys
        own_values = own_values + back_values
    dquery = (
        (
            inverse_rotary(grad_q.reshape(rows, local_heads, head_size), cosine_table, sine_table)
            * QUERY_SCALE
        )
        .astype(jnp.bfloat16)
        .reshape(rows, query_cols)
    )
    key_gradient = (
        inverse_rotary(own_keys.reshape(rows, local_groups, head_size), cosine_table, sine_table)
        .astype(jnp.bfloat16)
        .reshape(rows, key_value_columns)
    )
    value_gradient = own_values.astype(jnp.bfloat16)
    grads_qkv = jnp.concatenate([dquery, key_gradient, value_gradient], axis=1)
    partial_in = dot_rows(grads_qkv, full_qkv)
    in_grad = lax.psum_scatter(
        partial_in.astype(jnp.bfloat16), "head", scatter_dimension=1, tiled=True
    )
    grad_qkv_part = jnp.einsum("nd,nc->dc", hidden_in, grads_qkv, preferred_element_type=jnp.float32)
    grad_out_w = lax.psum_scatter(
        grad_w_out.astype(jnp.bfloat16), "ctx", scatter_dimension=0, tiled=True
    ).astype(jnp.float32)
    grad_qkv = lax.psum_scatter(
        grad_qkv_part.astype(jnp.bfloat16), "ctx", scatter_dimension=0, tiled=True
    ).astype(jnp.float32)
    grad_query = grad_qkv[:, :query_cols]
    grad_key = grad_qkv[:, query_cols : query_cols + key_value_columns]
    grad_value = grad_qkv[:, query_cols + key_value_columns :]
    return (in_grad, grad_query, grad_key, grad_value, grad_out_w)


def solution(mesh):
    in_specs = (
        P("ctx", None),
        P("ctx", None),
        P("ctx", "head"),
        P("ctx", "head"),
        P("ctx", "head"),
        P("ctx", "head"),
    )
    out_specs = (
        P("ctx", "head"),
        P("ctx", "head"),
        P("ctx", "head"),
        P("ctx", "head"),
        P("ctx", "head"),
    )
    return jax.shard_map(shards, mesh=mesh, in_specs=in_specs, out_specs=out_specs, check_vma=False)
```

```python
import jax
import jax.numpy as jnp
from jax import lax
from jax.sharding import PartitionSpec as P

HEAD_WIDTH = 128
WINDOW = 1024


QUERY_SCALE = 168.0 ** (-0.5)
ROPE_BASE = 10000.0
NEG_LARGE = -1e30


def from_behind(value, axis, steps):
    count = lax.axis_size(axis)
    initial, last = (max(0, -steps), min(count, count - steps))
    return lax.ppermute(value, axis, [(source, source + steps) for source in range(initial, last)])


def rope_tables(first, count, head_size):
    half = head_size // 2
    freq = ROPE_BASE ** (-(jnp.arange(half, dtype=jnp.float32) * 2.0 / head_size))
    places = first + jnp.arange(count, dtype=jnp.int32)
    angle = places.astype(jnp.float32)[:, None] * freq[None, :]
    return (jnp.cos(angle)[:, None, :], jnp.sin(angle)[:, None, :])


def apply_rotary(value_rows, cosine_table, sine_table):
    half = value_rows.shape[-1] // 2
    upper = value_rows[..., :half]
    lower = value_rows[..., half:]
    return jnp.concatenate(
        [upper * cosine_table - lower * sine_table, lower * cosine_table + upper * sine_table],
        axis=-1,
    )


def inverse_rotary(value_rows, cosine_table, sine_table):
    half = value_rows.shape[-1] // 2
    upper = value_rows[..., :half]
    lower = value_rows[..., half:]
    return jnp.concatenate(
        [upper * cosine_table + lower * sine_table, lower * cosine_table - upper * sine_table],
        axis=-1,
    )


def sum_over_heads(partial):
    count = lax.axis_size("head")
    me = lax.axis_index("head")
    rows, width = partial.shape
    blocks = partial.reshape(rows, count, width // count)
    total = lax.dynamic_index_in_dim(blocks, me, axis=1, keepdims=False).astype(jnp.float32)
    for shift in range(1, count):
        outgoing = lax.dynamic_index_in_dim(blocks, (me + shift) % count, axis=1, keepdims=False)
        incoming = lax.ppermute(
            outgoing, "head", [(source, (source + shift) % count) for source in range(count)]
        )
        total = total + incoming.astype(jnp.float32)
    return total.astype(jnp.bfloat16)

def dot_rows(left, weight):
    return lax.dot_general(
        left, weight, (((1,), (1,)), ((), ())), preferred_element_type=jnp.float32
    )


def attend_forward(query_rows, key_rows, value_rows, allowed):
    score = jnp.einsum("ngrd,mgd->grnm", query_rows, key_rows, preferred_element_type=jnp.float32)
    score = jnp.where(allowed[None, None], score, NEG_LARGE)
    top = jnp.max(score, axis=-1, keepdims=True)
    expo = jnp.exp(score - top)
    prob = expo / jnp.sum(expo, axis=-1, keepdims=True)
    prob_b = prob.astype(jnp.bfloat16)
    attended = jnp.einsum(
        "grnm,mgd->ngrd", prob_b, value_rows, preferred_element_type=jnp.float32
    ).astype(jnp.bfloat16)
    return (prob, prob_b, attended)


def attend_backward(prob, prob_b, attended, gradient_list, query_rows, key_rows, value_rows):
    delta = jnp.sum(gradient_list.astype(jnp.float32) * attended.astype(jnp.float32), axis=-1)
    delta = jnp.transpose(delta, (1, 2, 0))[..., None]
    grad_prob = jnp.einsum(
        "ngrd,mgd->grnm", gradient_list, value_rows, preferred_element_type=jnp.float32
    )
    grad_score = (prob * (grad_prob - delta)).astype(jnp.bfloat16)
    grad_q = jnp.einsum("grnm,mgd->ngrd", grad_score, key_rows, preferred_element_type=jnp.float32)
    grad_k = jnp.einsum(
        "grnm,ngrd->mgd", grad_score, query_rows, preferred_element_type=jnp.float32
    )
    grad_v = jnp.einsum("grnm,ngrd->mgd", prob_b, gradient_list, preferred_element_type=jnp.float32)
    return (grad_q, grad_k, grad_v)


def shards(hidden_in, out_grad, w_query, key_weight, value_weight, w_out):
    rows = hidden_in.shape[0]
    head_size = HEAD_WIDTH
    query_cols = w_query.shape[1]
    key_value_columns = key_weight.shape[1]
    local_heads = query_cols // head_size
    local_groups = key_value_columns // head_size
    group_ratio = local_heads // local_groups
    reach = WINDOW // rows
    first = lax.axis_index("ctx") * rows
    full_qkv = lax.all_gather(
        jnp.concatenate([w_query, key_weight, value_weight], axis=1), "ctx", axis=0, tiled=True
    )
    full_out = lax.all_gather(w_out, "ctx", axis=0, tiled=True)
    projected = jnp.dot(hidden_in, full_qkv, preferred_element_type=jnp.float32)
    query = projected[:, :query_cols]
    key_projected = projected[:, query_cols : query_cols + key_value_columns]
    value_projected = projected[:, query_cols + key_value_columns :]
    grad_att_f = jnp.dot(out_grad, full_out, preferred_element_type=jnp.float32)
    cosine_table, sine_table = rope_tables(first, rows, head_size)
    query_rows = (
        apply_rotary(query.reshape(rows, local_heads, head_size), cosine_table, sine_table)
        * QUERY_SCALE
    ).astype(jnp.bfloat16)
    keys_here = (
        apply_rotary(key_projected.reshape(rows, local_groups, head_size), cosine_table, sine_table)
        .astype(jnp.bfloat16)
        .reshape(rows, key_value_columns)
    )
    values_here = value_projected.astype(jnp.bfloat16)
    attention_gradient = grad_att_f.astype(jnp.bfloat16)
    key_blocks = []
    value_blocks = []
    for distance in range(reach, 0, -1):
        far_keys, far_values = from_behind((keys_here, values_here), "ctx", distance)
        key_blocks.append(far_keys)
        value_blocks.append(far_values)
    keys_all = jnp.concatenate(key_blocks + [keys_here], axis=0).reshape(
        -1, local_groups, head_size
    )
    values_all = jnp.concatenate(value_blocks + [values_here], axis=0).reshape(
        -1, local_groups, head_size
    )
    query_pos = first + jnp.arange(rows, dtype=jnp.int32)
    key_pos = first - reach * rows + jnp.arange((reach + 1) * rows, dtype=jnp.int32)
    allowed = (
        (key_pos[None, :] <= query_pos[:, None])
        & (key_pos[None, :] > query_pos[:, None] - WINDOW)
        & (key_pos[None, :] >= 0)
    )
    grouped_queries = query_rows.reshape(rows, local_groups, group_ratio, head_size)
    grouped_grads = attention_gradient.reshape(rows, local_groups, group_ratio, head_size)
    prob, prob_b, attended = attend_forward(grouped_queries, keys_all, values_all, allowed)
    attended_flat = attended.reshape(rows, query_cols)
    grad_w_out = jnp.einsum(
        "nd,nc->dc", out_grad, attended_flat, preferred_element_type=jnp.float32
    )
    grad_q, grad_k, grad_v = attend_backward(
        prob, prob_b, attended, grouped_grads, grouped_queries, keys_all, values_all
    )
    grad_k = grad_k.reshape(-1, key_value_columns)
    grad_v = grad_v.reshape(-1, key_value_columns)
    own_keys = grad_k[reach * rows :]
    own_values = grad_v[reach * rows :]
    for distance in range(1, reach + 1):
        lowest = (reach - distance) * rows
        back_keys, back_values = from_behind(
            (grad_k[lowest : lowest + rows], grad_v[lowest : lowest + rows]), "ctx", -distance
        )
        own_keys = own_keys + back_keys
        own_values = own_values + back_values
    dquery = (
        (
            inverse_rotary(grad_q.reshape(rows, local_heads, head_size), cosine_table, sine_table)
            * QUERY_SCALE
        )
        .astype(jnp.bfloat16)
        .reshape(rows, query_cols)
    )
    key_gradient = (
        inverse_rotary(own_keys.reshape(rows, local_groups, head_size), cosine_table, sine_table)
        .astype(jnp.bfloat16)
        .reshape(rows, key_value_columns)
    )
    value_gradient = own_values.astype(jnp.bfloat16)
    grads_qkv = jnp.concatenate([dquery, key_gradient, value_gradient], axis=1)
    partial_in = dot_rows(grads_qkv, full_qkv)
    in_grad = sum_over_heads(partial_in.astype(jnp.bfloat16))
    grad_qkv_part = jnp.einsum("nd,nc->dc", hidden_in, grads_qkv, preferred_element_type=jnp.float32)
    grad_out_w = lax.psum_scatter(
        grad_w_out.astype(jnp.bfloat16), "ctx", scatter_dimension=0, tiled=True
    ).astype(jnp.float32)
    grad_qkv = lax.psum_scatter(
        grad_qkv_part.astype(jnp.bfloat16), "ctx", scatter_dimension=0, tiled=True
    ).astype(jnp.float32)
    grad_query = grad_qkv[:, :query_cols]
    grad_key = grad_qkv[:, query_cols : query_cols + key_value_columns]
    grad_value = grad_qkv[:, query_cols + key_value_columns :]
    return (in_grad, grad_query, grad_key, grad_value, grad_out_w)


def solution(mesh):
    in_specs = (
        P("ctx", None),
        P("ctx", None),
        P("ctx", "head"),
        P("ctx", "head"),
        P("ctx", "head"),
        P("ctx", "head"),
    )
    out_specs = (
        P("ctx", "head"),
        P("ctx", "head"),
        P("ctx", "head"),
        P("ctx", "head"),
        P("ctx", "head"),
    )
    return jax.shard_map(shards, mesh=mesh, in_specs=in_specs, out_specs=out_specs, check_vma=False)
```

```python
import jax
import jax.numpy as jnp
from jax import lax
from jax.sharding import PartitionSpec as P
from jax.experimental.layout import Layout, with_layout_constraint

HEAD_WIDTH = 128
WINDOW = 1024


QUERY_SCALE = 168.0 ** (-0.5)
ROPE_BASE = 10000.0
NEG_LARGE = -1e30


def from_behind(value, axis, steps):
    count = lax.axis_size(axis)
    initial, last = (max(0, -steps), min(count, count - steps))
    return lax.ppermute(value, axis, [(source, source + steps) for source in range(initial, last)])


def rope_tables(first, count, head_size):
    half = head_size // 2
    freq = ROPE_BASE ** (-(jnp.arange(half, dtype=jnp.float32) * 2.0 / head_size))
    places = first + jnp.arange(count, dtype=jnp.int32)
    angle = places.astype(jnp.float32)[:, None] * freq[None, :]
    return (jnp.cos(angle)[:, None, :], jnp.sin(angle)[:, None, :])


def apply_rotary(value_rows, cosine_table, sine_table):
    half = value_rows.shape[-1] // 2
    upper = value_rows[..., :half]
    lower = value_rows[..., half:]
    return jnp.concatenate(
        [upper * cosine_table - lower * sine_table, lower * cosine_table + upper * sine_table],
        axis=-1,
    )


def inverse_rotary(value_rows, cosine_table, sine_table):
    half = value_rows.shape[-1] // 2
    upper = value_rows[..., :half]
    lower = value_rows[..., half:]
    return jnp.concatenate(
        [upper * cosine_table + lower * sine_table, lower * cosine_table - upper * sine_table],
        axis=-1,
    )


def sum_over_heads(partial):
    count = lax.axis_size("head")
    me = lax.axis_index("head")
    rows, width = partial.shape
    blocks = partial.reshape(rows, count, width // count)
    total = lax.dynamic_index_in_dim(blocks, me, axis=1, keepdims=False).astype(jnp.float32)
    for shift in range(1, count):
        outgoing = lax.dynamic_index_in_dim(blocks, (me + shift) % count, axis=1, keepdims=False)
        incoming = lax.ppermute(
            outgoing, "head", [(source, (source + shift) % count) for source in range(count)]
        )
        total = total + incoming.astype(jnp.float32)
    return total.astype(jnp.bfloat16)


def row_major(value):
    return with_layout_constraint(value, Layout(tuple(range(value.ndim))))

def dot_rows(left, weight):
    return lax.dot_general(
        left, weight, (((1,), (1,)), ((), ())), preferred_element_type=jnp.float32
    )


def attend_forward(query_rows, key_rows, value_rows, allowed):
    score = jnp.einsum("ngrd,mgd->grnm", query_rows, key_rows, preferred_element_type=jnp.float32)
    score = jnp.where(allowed[None, None], score, NEG_LARGE)
    top = jnp.max(score, axis=-1, keepdims=True)
    expo = jnp.exp(score - top)
    prob = expo / jnp.sum(expo, axis=-1, keepdims=True)
    prob_b = prob.astype(jnp.bfloat16)
    attended = jnp.einsum(
        "grnm,mgd->ngrd", prob_b, value_rows, preferred_element_type=jnp.float32
    ).astype(jnp.bfloat16)
    return (prob, prob_b, attended)


def attend_backward(prob, prob_b, attended, gradient_list, query_rows, key_rows, value_rows):
    delta = jnp.sum(gradient_list.astype(jnp.float32) * attended.astype(jnp.float32), axis=-1)
    delta = jnp.transpose(delta, (1, 2, 0))[..., None]
    grad_prob = jnp.einsum(
        "ngrd,mgd->grnm", gradient_list, value_rows, preferred_element_type=jnp.float32
    )
    grad_score = (prob * (grad_prob - delta)).astype(jnp.bfloat16)
    grad_q = jnp.einsum("grnm,mgd->ngrd", grad_score, key_rows, preferred_element_type=jnp.float32)
    grad_k = jnp.einsum(
        "grnm,ngrd->mgd", grad_score, query_rows, preferred_element_type=jnp.float32
    )
    grad_v = jnp.einsum("grnm,ngrd->mgd", prob_b, gradient_list, preferred_element_type=jnp.float32)
    return (grad_q, grad_k, grad_v)


def shards(hidden_in, out_grad, w_query, key_weight, value_weight, w_out):
    rows = hidden_in.shape[0]
    head_size = HEAD_WIDTH
    query_cols = w_query.shape[1]
    key_value_columns = key_weight.shape[1]
    local_heads = query_cols // head_size
    local_groups = key_value_columns // head_size
    group_ratio = local_heads // local_groups
    reach = WINDOW // rows
    first = lax.axis_index("ctx") * rows
    full_qkv = lax.all_gather(
        jnp.concatenate([w_query, key_weight, value_weight], axis=1), "ctx", axis=0, tiled=True
    )
    full_out = lax.all_gather(w_out, "ctx", axis=0, tiled=True)
    projected = jnp.dot(hidden_in, full_qkv, preferred_element_type=jnp.float32)
    query = projected[:, :query_cols]
    key_projected = projected[:, query_cols : query_cols + key_value_columns]
    value_projected = projected[:, query_cols + key_value_columns :]
    grad_att_f = jnp.dot(out_grad, full_out, preferred_element_type=jnp.float32)
    cosine_table, sine_table = rope_tables(first, rows, head_size)
    query_rows = (
        apply_rotary(query.reshape(rows, local_heads, head_size), cosine_table, sine_table)
        * QUERY_SCALE
    ).astype(jnp.bfloat16)
    keys_here = (
        apply_rotary(key_projected.reshape(rows, local_groups, head_size), cosine_table, sine_table)
        .astype(jnp.bfloat16)
        .reshape(rows, key_value_columns)
    )
    values_here = value_projected.astype(jnp.bfloat16)
    attention_gradient = grad_att_f.astype(jnp.bfloat16)
    key_blocks = []
    value_blocks = []
    for distance in range(reach, 0, -1):
        far_keys, far_values = from_behind((keys_here, values_here), "ctx", distance)
        key_blocks.append(far_keys)
        value_blocks.append(far_values)
    keys_all = jnp.concatenate(key_blocks + [keys_here], axis=0).reshape(
        -1, local_groups, head_size
    )
    values_all = jnp.concatenate(value_blocks + [values_here], axis=0).reshape(
        -1, local_groups, head_size
    )
    query_pos = first + jnp.arange(rows, dtype=jnp.int32)
    key_pos = first - reach * rows + jnp.arange((reach + 1) * rows, dtype=jnp.int32)
    allowed = (
        (key_pos[None, :] <= query_pos[:, None])
        & (key_pos[None, :] > query_pos[:, None] - WINDOW)
        & (key_pos[None, :] >= 0)
    )
    grouped_queries = query_rows.reshape(rows, local_groups, group_ratio, head_size)
    grouped_grads = attention_gradient.reshape(rows, local_groups, group_ratio, head_size)
    prob, prob_b, attended = attend_forward(grouped_queries, keys_all, values_all, allowed)
    attended_flat = attended.reshape(rows, query_cols)
    grad_w_out = jnp.einsum(
        "nd,nc->dc", out_grad, attended_flat, preferred_element_type=jnp.float32
    )
    grad_q, grad_k, grad_v = attend_backward(
        prob, prob_b, attended, grouped_grads, grouped_queries, keys_all, values_all
    )
    grad_k = grad_k.reshape(-1, key_value_columns)
    grad_v = grad_v.reshape(-1, key_value_columns)
    own_keys = grad_k[reach * rows :]
    own_values = grad_v[reach * rows :]
    for distance in range(1, reach + 1):
        lowest = (reach - distance) * rows
        back_keys, back_values = from_behind(
            (
                grad_k[lowest : lowest + rows].astype(jnp.bfloat16),
                grad_v[lowest : lowest + rows].astype(jnp.bfloat16),
            ),
            "ctx",
            -distance,
        )
        own_keys = own_keys + back_keys.astype(jnp.float32)
        own_values = own_values + back_values.astype(jnp.float32)
    dquery = (
        (
            inverse_rotary(grad_q.reshape(rows, local_heads, head_size), cosine_table, sine_table)
            * QUERY_SCALE
        )
        .astype(jnp.bfloat16)
        .reshape(rows, query_cols)
    )
    key_gradient = (
        inverse_rotary(own_keys.reshape(rows, local_groups, head_size), cosine_table, sine_table)
        .astype(jnp.bfloat16)
        .reshape(rows, key_value_columns)
    )
    value_gradient = own_values.astype(jnp.bfloat16)
    grads_qkv = jnp.concatenate([dquery, key_gradient, value_gradient], axis=1)
    partial_in = dot_rows(grads_qkv, full_qkv)
    in_grad = sum_over_heads(partial_in.astype(jnp.bfloat16))
    grad_qkv_part = jnp.einsum("nd,nc->dc", hidden_in, grads_qkv, preferred_element_type=jnp.float32)
    grad_out_w = lax.psum_scatter(
        row_major(grad_w_out.astype(jnp.bfloat16)), "ctx", scatter_dimension=0, tiled=True
    ).astype(jnp.float32)
    grad_qkv = lax.psum_scatter(
        row_major(grad_qkv_part.astype(jnp.bfloat16)), "ctx", scatter_dimension=0, tiled=True
    ).astype(jnp.float32)
    grad_query = grad_qkv[:, :query_cols]
    grad_key = grad_qkv[:, query_cols : query_cols + key_value_columns]
    grad_value = grad_qkv[:, query_cols + key_value_columns :]
    return (in_grad, grad_query, grad_key, grad_value, grad_out_w)


def solution(mesh):
    in_specs = (
        P("ctx", None),
        P("ctx", None),
        P("ctx", "head"),
        P("ctx", "head"),
        P("ctx", "head"),
        P("ctx", "head"),
    )
    out_specs = (
        P("ctx", "head"),
        P("ctx", "head"),
        P("ctx", "head"),
        P("ctx", "head"),
        P("ctx", "head"),
    )
    return jax.shard_map(shards, mesh=mesh, in_specs=in_specs, out_specs=out_specs, check_vma=False)
```

```python
import jax
import jax.numpy as jnp
from jax import lax
from jax.sharding import PartitionSpec as P
from jax.experimental.layout import Layout, with_layout_constraint

HEAD_WIDTH = 128
WINDOW = 1024


QUERY_SCALE = 168.0 ** (-0.5)
ROPE_BASE = 10000.0
NEG_LARGE = -1e30


def from_behind(value, axis, steps):
    count = lax.axis_size(axis)
    initial, last = (max(0, -steps), min(count, count - steps))
    return lax.ppermute(value, axis, [(source, source + steps) for source in range(initial, last)])


def rope_tables(first, count, head_size):
    half = head_size // 2
    freq = ROPE_BASE ** (-(jnp.arange(half, dtype=jnp.float32) * 2.0 / head_size))
    places = first + jnp.arange(count, dtype=jnp.int32)
    angle = places.astype(jnp.float32)[:, None] * freq[None, :]
    return (jnp.cos(angle)[:, None, :], jnp.sin(angle)[:, None, :])


def apply_rotary(value_rows, cosine_table, sine_table):
    half = value_rows.shape[-1] // 2
    upper = value_rows[..., :half]
    lower = value_rows[..., half:]
    return jnp.concatenate(
        [upper * cosine_table - lower * sine_table, lower * cosine_table + upper * sine_table],
        axis=-1,
    )


def inverse_rotary(value_rows, cosine_table, sine_table):
    half = value_rows.shape[-1] // 2
    upper = value_rows[..., :half]
    lower = value_rows[..., half:]
    return jnp.concatenate(
        [upper * cosine_table + lower * sine_table, lower * cosine_table - upper * sine_table],
        axis=-1,
    )


def sum_over_heads(partial):
    count = lax.axis_size("head")
    me = lax.axis_index("head")
    rows, width = partial.shape
    blocks = partial.reshape(rows, count, width // count)
    total = lax.dynamic_index_in_dim(blocks, me, axis=1, keepdims=False).astype(jnp.float32)
    for shift in range(1, count):
        outgoing = lax.dynamic_index_in_dim(blocks, (me + shift) % count, axis=1, keepdims=False)
        incoming = lax.ppermute(
            outgoing, "head", [(source, (source + shift) % count) for source in range(count)]
        )
        total = total + incoming.astype(jnp.float32)
    return total.astype(jnp.bfloat16)


def row_major(value):
    return with_layout_constraint(value, Layout(tuple(range(value.ndim))))

def dot_rows(left, weight):
    return lax.dot_general(
        left, weight, (((1,), (1,)), ((), ())), preferred_element_type=jnp.float32
    )


def attend_forward(query_rows, key_rows, value_rows, allowed):
    score = jnp.einsum("ngrd,mgd->grnm", query_rows, key_rows, preferred_element_type=jnp.float32)
    score = jnp.where(allowed[None, None], score, NEG_LARGE)
    top = jnp.max(score, axis=-1, keepdims=True)
    expo = jnp.exp(score - top)
    prob = expo / jnp.sum(expo, axis=-1, keepdims=True)
    prob_b = prob.astype(jnp.bfloat16)
    attended = jnp.einsum(
        "grnm,mgd->ngrd", prob_b, value_rows, preferred_element_type=jnp.float32
    ).astype(jnp.bfloat16)
    return (prob, prob_b, attended)


def attend_backward(prob, prob_b, attended, gradient_list, query_rows, key_rows, value_rows):
    delta = jnp.sum(gradient_list.astype(jnp.float32) * attended.astype(jnp.float32), axis=-1)
    delta = jnp.transpose(delta, (1, 2, 0))[..., None]
    grad_prob = jnp.einsum(
        "ngrd,mgd->grnm", gradient_list, value_rows, preferred_element_type=jnp.float32
    )
    grad_score = (prob * (grad_prob - delta)).astype(jnp.bfloat16)
    grad_q = jnp.einsum("grnm,mgd->ngrd", grad_score, key_rows, preferred_element_type=jnp.float32)
    grad_k = jnp.einsum(
        "grnm,ngrd->mgd", grad_score, query_rows, preferred_element_type=jnp.float32
    )
    grad_v = jnp.einsum("grnm,ngrd->mgd", prob_b, gradient_list, preferred_element_type=jnp.float32)
    return (grad_q, grad_k, grad_v)


def shards(hidden_in, out_grad, w_query, key_weight, value_weight, w_out):
    rows = hidden_in.shape[0]
    head_size = HEAD_WIDTH
    query_cols = w_query.shape[1]
    key_value_columns = key_weight.shape[1]
    local_heads = query_cols // head_size
    local_groups = key_value_columns // head_size
    group_ratio = local_heads // local_groups
    reach = WINDOW // rows
    first = lax.axis_index("ctx") * rows
    full_weights = lax.all_gather(
        jnp.concatenate([w_query, key_weight, value_weight, w_out], axis=1),
        "ctx",
        axis=0,
        tiled=True,
    )
    full_qkv = full_weights[:, : query_cols + 2 * key_value_columns]
    full_out = full_weights[:, query_cols + 2 * key_value_columns :]
    projected = jnp.dot(hidden_in, full_qkv, preferred_element_type=jnp.float32)
    query = projected[:, :query_cols]
    key_projected = projected[:, query_cols : query_cols + key_value_columns]
    value_projected = projected[:, query_cols + key_value_columns :]
    grad_att_f = jnp.dot(out_grad, full_out, preferred_element_type=jnp.float32)
    cosine_table, sine_table = rope_tables(first, rows, head_size)
    query_rows = (
        apply_rotary(query.reshape(rows, local_heads, head_size), cosine_table, sine_table)
        * QUERY_SCALE
    ).astype(jnp.bfloat16)
    keys_here = (
        apply_rotary(key_projected.reshape(rows, local_groups, head_size), cosine_table, sine_table)
        .astype(jnp.bfloat16)
        .reshape(rows, key_value_columns)
    )
    values_here = value_projected.astype(jnp.bfloat16)
    attention_gradient = grad_att_f.astype(jnp.bfloat16)
    key_blocks = []
    value_blocks = []
    for distance in range(reach, 0, -1):
        far_keys, far_values = from_behind((keys_here, values_here), "ctx", distance)
        key_blocks.append(far_keys)
        value_blocks.append(far_values)
    keys_all = jnp.concatenate(key_blocks + [keys_here], axis=0).reshape(
        -1, local_groups, head_size
    )
    values_all = jnp.concatenate(value_blocks + [values_here], axis=0).reshape(
        -1, local_groups, head_size
    )
    query_pos = first + jnp.arange(rows, dtype=jnp.int32)
    key_pos = first - reach * rows + jnp.arange((reach + 1) * rows, dtype=jnp.int32)
    allowed = (
        (key_pos[None, :] <= query_pos[:, None])
        & (key_pos[None, :] > query_pos[:, None] - WINDOW)
        & (key_pos[None, :] >= 0)
    )
    grouped_queries = query_rows.reshape(rows, local_groups, group_ratio, head_size)
    grouped_grads = attention_gradient.reshape(rows, local_groups, group_ratio, head_size)
    prob, prob_b, attended = attend_forward(grouped_queries, keys_all, values_all, allowed)
    attended_flat = attended.reshape(rows, query_cols)
    grad_w_out = jnp.einsum(
        "nd,nc->dc", out_grad, attended_flat, preferred_element_type=jnp.float32
    )
    grad_q, grad_k, grad_v = attend_backward(
        prob, prob_b, attended, grouped_grads, grouped_queries, keys_all, values_all
    )
    grad_k = grad_k.reshape(-1, key_value_columns)
    grad_v = grad_v.reshape(-1, key_value_columns)
    own_keys = grad_k[reach * rows :]
    own_values = grad_v[reach * rows :]
    for distance in range(1, reach + 1):
        lowest = (reach - distance) * rows
        back_keys, back_values = from_behind(
            (
                grad_k[lowest : lowest + rows].astype(jnp.bfloat16),
                grad_v[lowest : lowest + rows].astype(jnp.bfloat16),
            ),
            "ctx",
            -distance,
        )
        own_keys = own_keys + back_keys.astype(jnp.float32)
        own_values = own_values + back_values.astype(jnp.float32)
    dquery = (
        (
            inverse_rotary(grad_q.reshape(rows, local_heads, head_size), cosine_table, sine_table)
            * QUERY_SCALE
        )
        .astype(jnp.bfloat16)
        .reshape(rows, query_cols)
    )
    key_gradient = (
        inverse_rotary(own_keys.reshape(rows, local_groups, head_size), cosine_table, sine_table)
        .astype(jnp.bfloat16)
        .reshape(rows, key_value_columns)
    )
    value_gradient = own_values.astype(jnp.bfloat16)
    grads_qkv = jnp.concatenate([dquery, key_gradient, value_gradient], axis=1)
    partial_in = dot_rows(grads_qkv, full_qkv)
    in_grad = sum_over_heads(partial_in.astype(jnp.bfloat16))
    grad_qkv_part = jnp.einsum("nd,nc->dc", hidden_in, grads_qkv, preferred_element_type=jnp.float32)
    grad_out_w = lax.psum_scatter(
        row_major(grad_w_out.astype(jnp.bfloat16)), "ctx", scatter_dimension=0, tiled=True
    ).astype(jnp.float32)
    grad_qkv = lax.psum_scatter(
        row_major(grad_qkv_part.astype(jnp.bfloat16)), "ctx", scatter_dimension=0, tiled=True
    ).astype(jnp.float32)
    grad_query = grad_qkv[:, :query_cols]
    grad_key = grad_qkv[:, query_cols : query_cols + key_value_columns]
    grad_value = grad_qkv[:, query_cols + key_value_columns :]
    return (in_grad, grad_query, grad_key, grad_value, grad_out_w)


def solution(mesh):
    in_specs = (
        P("ctx", None),
        P("ctx", None),
        P("ctx", "head"),
        P("ctx", "head"),
        P("ctx", "head"),
        P("ctx", "head"),
    )
    out_specs = (
        P("ctx", "head"),
        P("ctx", "head"),
        P("ctx", "head"),
        P("ctx", "head"),
        P("ctx", "head"),
    )
    return jax.shard_map(shards, mesh=mesh, in_specs=in_specs, out_specs=out_specs, check_vma=False)
```

```python
import jax
import jax.numpy as jnp
from jax import lax
from jax.sharding import PartitionSpec as P
from jax.experimental.layout import Layout, with_layout_constraint

HEAD_WIDTH = 128
WINDOW = 1024


QUERY_SCALE = 168.0 ** (-0.5)
ROPE_BASE = 10000.0
NEG_LARGE = -1e30


def from_behind(value, axis, steps):
    count = lax.axis_size(axis)
    initial, last = (max(0, -steps), min(count, count - steps))
    return lax.ppermute(value, axis, [(source, source + steps) for source in range(initial, last)])


def rope_tables(first, count, head_size):
    half = head_size // 2
    freq = ROPE_BASE ** (-(jnp.arange(half, dtype=jnp.float32) * 2.0 / head_size))
    places = first + jnp.arange(count, dtype=jnp.int32)
    angle = places.astype(jnp.float32)[:, None] * freq[None, :]
    return (jnp.cos(angle)[:, None, :], jnp.sin(angle)[:, None, :])


def apply_rotary(value_rows, cosine_table, sine_table):
    half = value_rows.shape[-1] // 2
    upper = value_rows[..., :half]
    lower = value_rows[..., half:]
    return jnp.concatenate(
        [upper * cosine_table - lower * sine_table, lower * cosine_table + upper * sine_table],
        axis=-1,
    )


def inverse_rotary(value_rows, cosine_table, sine_table):
    half = value_rows.shape[-1] // 2
    upper = value_rows[..., :half]
    lower = value_rows[..., half:]
    return jnp.concatenate(
        [upper * cosine_table + lower * sine_table, lower * cosine_table - upper * sine_table],
        axis=-1,
    )


def sum_over_heads(partial):
    count = lax.axis_size("head")
    me = lax.axis_index("head")
    rows, width = partial.shape
    blocks = partial.reshape(rows, count, width // count)
    total = lax.dynamic_index_in_dim(blocks, me, axis=1, keepdims=False).astype(jnp.float32)
    for shift in range(1, count):
        outgoing = lax.dynamic_index_in_dim(blocks, (me + shift) % count, axis=1, keepdims=False)
        incoming = lax.ppermute(
            outgoing, "head", [(source, (source + shift) % count) for source in range(count)]
        )
        total = total + incoming.astype(jnp.float32)
    return total.astype(jnp.bfloat16)


def row_major(value):
    return with_layout_constraint(value, Layout(tuple(range(value.ndim))))

def dot_rows(left, weight):
    return lax.dot_general(
        left, weight, (((1,), (1,)), ((), ())), preferred_element_type=jnp.float32
    )


def attend_forward(query_rows, key_rows, value_rows, allowed):
    score = jnp.einsum("ngrd,mgd->grnm", query_rows, key_rows, preferred_element_type=jnp.float32)
    score = jnp.where(allowed[None, None], score, NEG_LARGE)
    top = jnp.max(score, axis=-1, keepdims=True)
    expo = jnp.exp(score - top)
    prob = expo / jnp.sum(expo, axis=-1, keepdims=True)
    prob_b = prob.astype(jnp.bfloat16)
    attended = jnp.einsum(
        "grnm,mgd->ngrd", prob_b, value_rows, preferred_element_type=jnp.float32
    ).astype(jnp.bfloat16)
    return (prob, prob_b, attended)


def attend_backward(prob, prob_b, attended, gradient_list, query_rows, key_rows, value_rows):
    delta = jnp.sum(gradient_list.astype(jnp.float32) * attended.astype(jnp.float32), axis=-1)
    delta = jnp.transpose(delta, (1, 2, 0))[..., None]
    grad_prob = jnp.einsum(
        "ngrd,mgd->grnm", gradient_list, value_rows, preferred_element_type=jnp.float32
    )
    grad_score = (prob * (grad_prob - delta)).astype(jnp.bfloat16)
    grad_q = jnp.einsum("grnm,mgd->ngrd", grad_score, key_rows, preferred_element_type=jnp.float32)
    grad_k = jnp.einsum(
        "grnm,ngrd->mgd", grad_score, query_rows, preferred_element_type=jnp.float32
    )
    grad_v = jnp.einsum("grnm,ngrd->mgd", prob_b, gradient_list, preferred_element_type=jnp.float32)
    return (grad_q, grad_k, grad_v)


def shards(hidden_in, out_grad, w_query, key_weight, value_weight, w_out):
    rows = hidden_in.shape[0]
    head_size = HEAD_WIDTH
    query_cols = w_query.shape[1]
    key_value_columns = key_weight.shape[1]
    local_heads = query_cols // head_size
    local_groups = key_value_columns // head_size
    group_ratio = local_heads // local_groups
    reach = WINDOW // rows
    first = lax.axis_index("ctx") * rows
    full_qkv = lax.all_gather(
        jnp.concatenate([w_query, key_weight, value_weight], axis=1), "ctx", axis=0, tiled=True
    )
    full_out = lax.all_gather(w_out, "ctx", axis=0, tiled=True)
    projected = jnp.dot(hidden_in, full_qkv, preferred_element_type=jnp.float32)
    query = projected[:, :query_cols]
    key_projected = projected[:, query_cols : query_cols + key_value_columns]
    value_projected = projected[:, query_cols + key_value_columns :]
    cosine_table, sine_table = rope_tables(first, rows, head_size)
    query_rows = (
        apply_rotary(query.reshape(rows, local_heads, head_size), cosine_table, sine_table)
        * QUERY_SCALE
    ).astype(jnp.bfloat16)
    keys_here = (
        apply_rotary(key_projected.reshape(rows, local_groups, head_size), cosine_table, sine_table)
        .astype(jnp.bfloat16)
        .reshape(rows, key_value_columns)
    )
    values_here = value_projected.astype(jnp.bfloat16)
    key_blocks = []
    value_blocks = []
    for distance in range(reach, 0, -1):
        far_keys, far_values = from_behind((keys_here, values_here), "ctx", distance)
        key_blocks.append(far_keys)
        value_blocks.append(far_values)
    keys_all = jnp.concatenate(key_blocks + [keys_here], axis=0).reshape(
        -1, local_groups, head_size
    )
    values_all = jnp.concatenate(value_blocks + [values_here], axis=0).reshape(
        -1, local_groups, head_size
    )
    query_pos = first + jnp.arange(rows, dtype=jnp.int32)
    key_pos = first - reach * rows + jnp.arange((reach + 1) * rows, dtype=jnp.int32)
    allowed = (
        (key_pos[None, :] <= query_pos[:, None])
        & (key_pos[None, :] > query_pos[:, None] - WINDOW)
        & (key_pos[None, :] >= 0)
    )
    grouped_queries = query_rows.reshape(rows, local_groups, group_ratio, head_size)
    prob, prob_b, attended = attend_forward(grouped_queries, keys_all, values_all, allowed)
    attended, late_out_grad = lax.optimization_barrier((attended, out_grad))
    attention_gradient = jnp.dot(
        late_out_grad, full_out, preferred_element_type=jnp.float32
    ).astype(jnp.bfloat16)
    grouped_grads = attention_gradient.reshape(rows, local_groups, group_ratio, head_size)
    attended_flat = attended.reshape(rows, query_cols)
    grad_w_out = jnp.einsum(
        "nd,nc->dc", out_grad, attended_flat, preferred_element_type=jnp.float32
    )
    grad_q, grad_k, grad_v = attend_backward(
        prob, prob_b, attended, grouped_grads, grouped_queries, keys_all, values_all
    )
    grad_k = grad_k.reshape(-1, key_value_columns)
    grad_v = grad_v.reshape(-1, key_value_columns)
    own_keys = grad_k[reach * rows :]
    own_values = grad_v[reach * rows :]
    for distance in range(1, reach + 1):
        lowest = (reach - distance) * rows
        back_keys, back_values = from_behind(
            (
                grad_k[lowest : lowest + rows].astype(jnp.bfloat16),
                grad_v[lowest : lowest + rows].astype(jnp.bfloat16),
            ),
            "ctx",
            -distance,
        )
        own_keys = own_keys + back_keys.astype(jnp.float32)
        own_values = own_values + back_values.astype(jnp.float32)
    dquery = (
        (
            inverse_rotary(grad_q.reshape(rows, local_heads, head_size), cosine_table, sine_table)
            * QUERY_SCALE
        )
        .astype(jnp.bfloat16)
        .reshape(rows, query_cols)
    )
    key_gradient = (
        inverse_rotary(own_keys.reshape(rows, local_groups, head_size), cosine_table, sine_table)
        .astype(jnp.bfloat16)
        .reshape(rows, key_value_columns)
    )
    value_gradient = own_values.astype(jnp.bfloat16)
    grads_qkv = jnp.concatenate([dquery, key_gradient, value_gradient], axis=1)
    partial_in = dot_rows(grads_qkv, full_qkv)
    in_grad = sum_over_heads(partial_in.astype(jnp.bfloat16))
    grad_qkv_part = jnp.einsum("nd,nc->dc", hidden_in, grads_qkv, preferred_element_type=jnp.float32)
    grad_out_w = lax.psum_scatter(
        row_major(grad_w_out.astype(jnp.bfloat16)), "ctx", scatter_dimension=0, tiled=True
    ).astype(jnp.float32)
    grad_qkv = lax.psum_scatter(
        row_major(grad_qkv_part.astype(jnp.bfloat16)), "ctx", scatter_dimension=0, tiled=True
    ).astype(jnp.float32)
    grad_query = grad_qkv[:, :query_cols]
    grad_key = grad_qkv[:, query_cols : query_cols + key_value_columns]
    grad_value = grad_qkv[:, query_cols + key_value_columns :]
    return (in_grad, grad_query, grad_key, grad_value, grad_out_w)


def solution(mesh):
    in_specs = (
        P("ctx", None),
        P("ctx", None),
        P("ctx", "head"),
        P("ctx", "head"),
        P("ctx", "head"),
        P("ctx", "head"),
    )
    out_specs = (
        P("ctx", "head"),
        P("ctx", "head"),
        P("ctx", "head"),
        P("ctx", "head"),
        P("ctx", "head"),
    )
    return jax.shard_map(shards, mesh=mesh, in_specs=in_specs, out_specs=out_specs, check_vma=False)
```

```python
import jax
import jax.numpy as jnp
from jax import lax
from jax.sharding import PartitionSpec as P
from jax.experimental.layout import Layout, with_layout_constraint

HEAD_WIDTH = 128
WINDOW = 1024


QUERY_SCALE = 168.0 ** (-0.5)
ROPE_BASE = 10000.0
NEG_LARGE = -1e30


def from_behind(value, axis, steps):
    count = lax.axis_size(axis)
    initial, last = (max(0, -steps), min(count, count - steps))
    return lax.ppermute(value, axis, [(source, source + steps) for source in range(initial, last)])


def rope_tables(first, count, head_size):
    half = head_size // 2
    freq = ROPE_BASE ** (-(jnp.arange(half, dtype=jnp.float32) * 2.0 / head_size))
    places = first + jnp.arange(count, dtype=jnp.int32)
    angle = places.astype(jnp.float32)[:, None] * freq[None, :]
    return (jnp.cos(angle)[:, None, :], jnp.sin(angle)[:, None, :])


def apply_rotary(value_rows, cosine_table, sine_table):
    half = value_rows.shape[-1] // 2
    upper = value_rows[..., :half]
    lower = value_rows[..., half:]
    return jnp.concatenate(
        [upper * cosine_table - lower * sine_table, lower * cosine_table + upper * sine_table],
        axis=-1,
    )


def inverse_rotary(value_rows, cosine_table, sine_table):
    half = value_rows.shape[-1] // 2
    upper = value_rows[..., :half]
    lower = value_rows[..., half:]
    return jnp.concatenate(
        [upper * cosine_table + lower * sine_table, lower * cosine_table - upper * sine_table],
        axis=-1,
    )


def sum_over_heads(partial):
    count = lax.axis_size("head")
    me = lax.axis_index("head")
    rows, width = partial.shape
    blocks = partial.reshape(rows, count, width // count)
    total = lax.dynamic_index_in_dim(blocks, me, axis=1, keepdims=False).astype(jnp.float32)
    for shift in range(1, count):
        outgoing = lax.dynamic_index_in_dim(blocks, (me + shift) % count, axis=1, keepdims=False)
        incoming = lax.ppermute(
            outgoing, "head", [(source, (source + shift) % count) for source in range(count)]
        )
        total = total + incoming.astype(jnp.float32)
    return total.astype(jnp.bfloat16)


def row_major(value):
    return with_layout_constraint(value, Layout(tuple(range(value.ndim))))

def dot_rows(left, weight):
    return lax.dot_general(
        left, weight, (((1,), (1,)), ((), ())), preferred_element_type=jnp.float32
    )


def attend_forward(query_rows, key_rows, value_rows, allowed):
    score = jnp.einsum("ngrd,mgd->grnm", query_rows, key_rows, preferred_element_type=jnp.float32)
    score = jnp.where(allowed[None, None], score, NEG_LARGE)
    top = jnp.max(score, axis=-1, keepdims=True)
    expo = jnp.exp(score - top)
    prob = expo / jnp.sum(expo, axis=-1, keepdims=True)
    prob_b = prob.astype(jnp.bfloat16)
    attended = jnp.einsum(
        "grnm,mgd->ngrd", prob_b, value_rows, preferred_element_type=jnp.float32
    ).astype(jnp.bfloat16)
    return (prob, prob_b, attended)


def attend_backward(prob, prob_b, attended, gradient_list, query_rows, key_rows, value_rows, block):
    delta = jnp.sum(gradient_list.astype(jnp.float32) * attended.astype(jnp.float32), axis=-1)
    delta = jnp.transpose(delta, (1, 2, 0))[..., None]
    grad_prob = jnp.einsum(
        "ngrd,mgd->grnm", gradient_list, value_rows, preferred_element_type=jnp.float32
    )
    grad_score = (prob * (grad_prob - delta)).astype(jnp.bfloat16)
    grad_q = jnp.einsum("grnm,mgd->ngrd", grad_score, key_rows, preferred_element_type=jnp.float32)
    grad_k = []
    grad_v = []
    for lowest in range(0, key_rows.shape[0], block):
        grad_k.append(
            jnp.einsum(
                "grnm,ngrd->mgd",
                grad_score[..., lowest : lowest + block],
                query_rows,
                preferred_element_type=jnp.float32,
            )
        )
        grad_v.append(
            jnp.einsum(
                "grnm,ngrd->mgd",
                prob_b[..., lowest : lowest + block],
                gradient_list,
                preferred_element_type=jnp.float32,
            )
        )
    return (grad_q, grad_k, grad_v)


def shards(hidden_in, out_grad, w_query, key_weight, value_weight, w_out):
    rows = hidden_in.shape[0]
    head_size = HEAD_WIDTH
    query_cols = w_query.shape[1]
    key_value_columns = key_weight.shape[1]
    local_heads = query_cols // head_size
    local_groups = key_value_columns // head_size
    group_ratio = local_heads // local_groups
    reach = WINDOW // rows
    first = lax.axis_index("ctx") * rows
    full_qkv = lax.all_gather(
        jnp.concatenate([w_query, key_weight, value_weight], axis=1), "ctx", axis=0, tiled=True
    )
    full_out = lax.all_gather(w_out, "ctx", axis=0, tiled=True)
    projected = jnp.dot(hidden_in, full_qkv, preferred_element_type=jnp.float32)
    query = projected[:, :query_cols]
    key_projected = projected[:, query_cols : query_cols + key_value_columns]
    value_projected = projected[:, query_cols + key_value_columns :]
    cosine_table, sine_table = rope_tables(first, rows, head_size)
    query_rows = (
        apply_rotary(query.reshape(rows, local_heads, head_size), cosine_table, sine_table)
        * QUERY_SCALE
    ).astype(jnp.bfloat16)
    keys_here = (
        apply_rotary(key_projected.reshape(rows, local_groups, head_size), cosine_table, sine_table)
        .astype(jnp.bfloat16)
        .reshape(rows, key_value_columns)
    )
    values_here = value_projected.astype(jnp.bfloat16)
    key_blocks = []
    value_blocks = []
    for distance in range(reach, 0, -1):
        far_keys, far_values = from_behind((keys_here, values_here), "ctx", distance)
        key_blocks.append(far_keys)
        value_blocks.append(far_values)
    keys_all = jnp.concatenate(key_blocks + [keys_here], axis=0).reshape(
        -1, local_groups, head_size
    )
    values_all = jnp.concatenate(value_blocks + [values_here], axis=0).reshape(
        -1, local_groups, head_size
    )
    query_pos = first + jnp.arange(rows, dtype=jnp.int32)
    key_pos = first - reach * rows + jnp.arange((reach + 1) * rows, dtype=jnp.int32)
    allowed = (
        (key_pos[None, :] <= query_pos[:, None])
        & (key_pos[None, :] > query_pos[:, None] - WINDOW)
        & (key_pos[None, :] >= 0)
    )
    grouped_queries = query_rows.reshape(rows, local_groups, group_ratio, head_size)
    prob, prob_b, attended = attend_forward(grouped_queries, keys_all, values_all, allowed)
    attended, late_out_grad = lax.optimization_barrier((attended, out_grad))
    attention_gradient = jnp.dot(
        late_out_grad, full_out, preferred_element_type=jnp.float32
    ).astype(jnp.bfloat16)
    grouped_grads = attention_gradient.reshape(rows, local_groups, group_ratio, head_size)
    attended_flat = attended.reshape(rows, query_cols)
    grad_w_out = jnp.einsum(
        "nd,nc->dc", out_grad, attended_flat, preferred_element_type=jnp.float32
    )
    grad_q, grad_k, grad_v = attend_backward(
        prob, prob_b, attended, grouped_grads, grouped_queries, keys_all, values_all, rows
    )
    grad_k = [part.reshape(rows, key_value_columns) for part in grad_k]
    grad_v = [part.reshape(rows, key_value_columns) for part in grad_v]
    own_keys = grad_k[reach]
    own_values = grad_v[reach]
    for distance in range(1, reach + 1):
        back_keys, back_values = from_behind(
            (
                grad_k[reach - distance].astype(jnp.bfloat16),
                grad_v[reach - distance].astype(jnp.bfloat16),
            ),
            "ctx",
            -distance,
        )
        own_keys = own_keys + back_keys.astype(jnp.float32)
        own_values = own_values + back_values.astype(jnp.float32)
    dquery = (
        (
            inverse_rotary(grad_q.reshape(rows, local_heads, head_size), cosine_table, sine_table)
            * QUERY_SCALE
        )
        .astype(jnp.bfloat16)
        .reshape(rows, query_cols)
    )
    key_gradient = (
        inverse_rotary(own_keys.reshape(rows, local_groups, head_size), cosine_table, sine_table)
        .astype(jnp.bfloat16)
        .reshape(rows, key_value_columns)
    )
    value_gradient = own_values.astype(jnp.bfloat16)
    grads_qkv = jnp.concatenate([dquery, key_gradient, value_gradient], axis=1)
    partial_in = dot_rows(grads_qkv, full_qkv)
    in_grad = sum_over_heads(partial_in.astype(jnp.bfloat16))
    grad_qkv_part = jnp.einsum("nd,nc->dc", hidden_in, grads_qkv, preferred_element_type=jnp.float32)
    grad_out_w = lax.psum_scatter(
        row_major(grad_w_out.astype(jnp.bfloat16)), "ctx", scatter_dimension=0, tiled=True
    ).astype(jnp.float32)
    grad_qkv = lax.psum_scatter(
        row_major(grad_qkv_part.astype(jnp.bfloat16)), "ctx", scatter_dimension=0, tiled=True
    ).astype(jnp.float32)
    grad_query = grad_qkv[:, :query_cols]
    grad_key = grad_qkv[:, query_cols : query_cols + key_value_columns]
    grad_value = grad_qkv[:, query_cols + key_value_columns :]
    return (in_grad, grad_query, grad_key, grad_value, grad_out_w)


def solution(mesh):
    in_specs = (
        P("ctx", None),
        P("ctx", None),
        P("ctx", "head"),
        P("ctx", "head"),
        P("ctx", "head"),
        P("ctx", "head"),
    )
    out_specs = (
        P("ctx", "head"),
        P("ctx", "head"),
        P("ctx", "head"),
        P("ctx", "head"),
        P("ctx", "head"),
    )
    return jax.shard_map(shards, mesh=mesh, in_specs=in_specs, out_specs=out_specs, check_vma=False)
```

```python
import jax
import jax.numpy as jnp
from jax import lax
from jax.sharding import PartitionSpec as P
from jax.experimental.layout import Layout, with_layout_constraint

HEAD_WIDTH = 128
WINDOW = 1024


QUERY_SCALE = 168.0 ** (-0.5)
ROPE_BASE = 10000.0
NEG_LARGE = -1e30


def from_behind(value, axis, steps):
    count = lax.axis_size(axis)
    initial, last = (max(0, -steps), min(count, count - steps))
    return lax.ppermute(value, axis, [(source, source + steps) for source in range(initial, last)])


def rope_tables(first, count, head_size):
    half = head_size // 2
    freq = ROPE_BASE ** (-(jnp.arange(half, dtype=jnp.float32) * 2.0 / head_size))
    places = first + jnp.arange(count, dtype=jnp.int32)
    angle = places.astype(jnp.float32)[:, None] * freq[None, :]
    return (jnp.cos(angle)[:, None, :], jnp.sin(angle)[:, None, :])


def apply_rotary(value_rows, cosine_table, sine_table):
    half = value_rows.shape[-1] // 2
    upper = value_rows[..., :half]
    lower = value_rows[..., half:]
    return jnp.concatenate(
        [upper * cosine_table - lower * sine_table, lower * cosine_table + upper * sine_table],
        axis=-1,
    )


def inverse_rotary(value_rows, cosine_table, sine_table):
    half = value_rows.shape[-1] // 2
    upper = value_rows[..., :half]
    lower = value_rows[..., half:]
    return jnp.concatenate(
        [upper * cosine_table + lower * sine_table, lower * cosine_table - upper * sine_table],
        axis=-1,
    )


def sum_over_heads(partial):
    count = lax.axis_size("head")
    me = lax.axis_index("head")
    rows, width = partial.shape
    blocks = partial.reshape(rows, count, width // count)
    total = lax.dynamic_index_in_dim(blocks, me, axis=1, keepdims=False).astype(jnp.float32)
    for shift in range(1, count):
        outgoing = lax.dynamic_index_in_dim(blocks, (me + shift) % count, axis=1, keepdims=False)
        incoming = lax.ppermute(
            outgoing, "head", [(source, (source + shift) % count) for source in range(count)]
        )
        total = total + incoming.astype(jnp.float32)
    return total.astype(jnp.bfloat16)


def row_major(value):
    return with_layout_constraint(value, Layout(tuple(range(value.ndim))))

def dot_rows(left, weight):
    return lax.dot_general(
        left, weight, (((1,), (1,)), ((), ())), preferred_element_type=jnp.float32
    )


def attend_forward(query_rows, key_rows, value_rows, allowed):
    score = jnp.einsum("ngrd,mgd->grnm", query_rows, key_rows, preferred_element_type=jnp.float32)
    score = jnp.where(allowed[None, None], score, NEG_LARGE)
    top = jnp.max(score, axis=-1, keepdims=True)
    expo = jnp.exp(score - top)
    prob = expo / jnp.sum(expo, axis=-1, keepdims=True)
    prob_b = prob.astype(jnp.bfloat16)
    attended = jnp.einsum(
        "grnm,mgd->ngrd", prob_b, value_rows, preferred_element_type=jnp.float32
    ).astype(jnp.bfloat16)
    return (prob, prob_b, attended)


def attend_backward(prob, prob_b, attended, gradient_list, query_rows, key_rows, value_rows, block):
    delta = jnp.sum(gradient_list.astype(jnp.float32) * attended.astype(jnp.float32), axis=-1)
    delta = jnp.transpose(delta, (1, 2, 0))[..., None]
    grad_prob = jnp.einsum(
        "ngrd,mgd->grnm", gradient_list, value_rows, preferred_element_type=jnp.float32
    )
    grad_score = (prob * (grad_prob - delta)).astype(jnp.bfloat16)
    grad_q = jnp.einsum("grnm,mgd->ngrd", grad_score, key_rows, preferred_element_type=jnp.float32)
    grad_k = []
    grad_v = []
    for lowest in range(0, key_rows.shape[0], block):
        grad_k.append(
            jnp.einsum(
                "grnm,ngrd->mgd",
                grad_score[..., lowest : lowest + block],
                query_rows,
                preferred_element_type=jnp.float32,
            )
        )
        grad_v.append(
            jnp.einsum(
                "grnm,ngrd->mgd",
                prob_b[..., lowest : lowest + block],
                gradient_list,
                preferred_element_type=jnp.float32,
            )
        )
    return (grad_q, grad_k, grad_v)


def shards(hidden_in, out_grad, w_query, key_weight, value_weight, w_out):
    rows = hidden_in.shape[0]
    head_size = HEAD_WIDTH
    query_cols = w_query.shape[1]
    key_value_columns = key_weight.shape[1]
    local_heads = query_cols // head_size
    local_groups = key_value_columns // head_size
    group_ratio = local_heads // local_groups
    reach = WINDOW // rows
    first = lax.axis_index("ctx") * rows
    full_qkv = lax.all_gather(
        jnp.concatenate([w_query, key_weight, value_weight], axis=1), "ctx", axis=0, tiled=True
    )
    full_out = lax.all_gather(w_out, "ctx", axis=0, tiled=True)
    projected = jnp.dot(hidden_in, full_qkv, preferred_element_type=jnp.float32)
    query = projected[:, :query_cols]
    key_projected = projected[:, query_cols : query_cols + key_value_columns]
    value_projected = projected[:, query_cols + key_value_columns :]
    cosine_table, sine_table = rope_tables(first, rows, head_size)
    query_rows = (
        apply_rotary(query.reshape(rows, local_heads, head_size), cosine_table, sine_table)
        * QUERY_SCALE
    ).astype(jnp.bfloat16)
    keys_here = (
        apply_rotary(key_projected.reshape(rows, local_groups, head_size), cosine_table, sine_table)
        .astype(jnp.bfloat16)
        .reshape(rows, key_value_columns)
    )
    values_here = value_projected.astype(jnp.bfloat16)
    key_blocks = []
    value_blocks = []
    for distance in range(reach, 0, -1):
        far = from_behind(jnp.concatenate([keys_here, values_here], axis=1), "ctx", distance)
        key_blocks.append(far[:, :key_value_columns])
        value_blocks.append(far[:, key_value_columns:])
    keys_all = jnp.concatenate(key_blocks + [keys_here], axis=0).reshape(
        -1, local_groups, head_size
    )
    values_all = jnp.concatenate(value_blocks + [values_here], axis=0).reshape(
        -1, local_groups, head_size
    )
    query_pos = first + jnp.arange(rows, dtype=jnp.int32)
    key_pos = first - reach * rows + jnp.arange((reach + 1) * rows, dtype=jnp.int32)
    allowed = (
        (key_pos[None, :] <= query_pos[:, None])
        & (key_pos[None, :] > query_pos[:, None] - WINDOW)
        & (key_pos[None, :] >= 0)
    )
    grouped_queries = query_rows.reshape(rows, local_groups, group_ratio, head_size)
    prob, prob_b, attended = attend_forward(grouped_queries, keys_all, values_all, allowed)
    attended, late_out_grad = lax.optimization_barrier((attended, out_grad))
    attention_gradient = jnp.dot(
        late_out_grad, full_out, preferred_element_type=jnp.float32
    ).astype(jnp.bfloat16)
    grouped_grads = attention_gradient.reshape(rows, local_groups, group_ratio, head_size)
    attended_flat = attended.reshape(rows, query_cols)
    grad_w_out = jnp.einsum(
        "nd,nc->dc", out_grad, attended_flat, preferred_element_type=jnp.float32
    )
    grad_q, grad_k, grad_v = attend_backward(
        prob, prob_b, attended, grouped_grads, grouped_queries, keys_all, values_all, rows
    )
    grad_k = [part.reshape(rows, key_value_columns) for part in grad_k]
    grad_v = [part.reshape(rows, key_value_columns) for part in grad_v]
    own_keys = grad_k[reach]
    own_values = grad_v[reach]
    for distance in range(1, reach + 1):
        back = from_behind(
            jnp.concatenate([grad_k[reach - distance], grad_v[reach - distance]], axis=1).astype(
                jnp.bfloat16
            ),
            "ctx",
            -distance,
        )
        back_keys = back[:, :key_value_columns]
        back_values = back[:, key_value_columns:]
        own_keys = own_keys + back_keys.astype(jnp.float32)
        own_values = own_values + back_values.astype(jnp.float32)
    dquery = (
        (
            inverse_rotary(grad_q.reshape(rows, local_heads, head_size), cosine_table, sine_table)
            * QUERY_SCALE
        )
        .astype(jnp.bfloat16)
        .reshape(rows, query_cols)
    )
    key_gradient = (
        inverse_rotary(own_keys.reshape(rows, local_groups, head_size), cosine_table, sine_table)
        .astype(jnp.bfloat16)
        .reshape(rows, key_value_columns)
    )
    value_gradient = own_values.astype(jnp.bfloat16)
    grads_qkv = jnp.concatenate([dquery, key_gradient, value_gradient], axis=1)
    partial_in = dot_rows(grads_qkv, full_qkv)
    in_grad = sum_over_heads(partial_in.astype(jnp.bfloat16))
    grad_qkv_part = jnp.einsum("nd,nc->dc", hidden_in, grads_qkv, preferred_element_type=jnp.float32)
    grad_out_w = lax.psum_scatter(
        row_major(grad_w_out.astype(jnp.bfloat16)), "ctx", scatter_dimension=0, tiled=True
    ).astype(jnp.float32)
    grad_qkv = lax.psum_scatter(
        row_major(grad_qkv_part.astype(jnp.bfloat16)), "ctx", scatter_dimension=0, tiled=True
    ).astype(jnp.float32)
    grad_query = grad_qkv[:, :query_cols]
    grad_key = grad_qkv[:, query_cols : query_cols + key_value_columns]
    grad_value = grad_qkv[:, query_cols + key_value_columns :]
    return (in_grad, grad_query, grad_key, grad_value, grad_out_w)


def solution(mesh):
    in_specs = (
        P("ctx", None),
        P("ctx", None),
        P("ctx", "head"),
        P("ctx", "head"),
        P("ctx", "head"),
        P("ctx", "head"),
    )
    out_specs = (
        P("ctx", "head"),
        P("ctx", "head"),
        P("ctx", "head"),
        P("ctx", "head"),
        P("ctx", "head"),
    )
    return jax.shard_map(shards, mesh=mesh, in_specs=in_specs, out_specs=out_specs, check_vma=False)
```

```python
import jax
import jax.numpy as jnp
from jax import lax
from jax.sharding import PartitionSpec as P
from jax.experimental.layout import Layout, with_layout_constraint

HEAD_WIDTH = 128
WINDOW = 1024


QUERY_SCALE = 168.0 ** (-0.5)
ROPE_BASE = 10000.0
NEG_LARGE = -1e30


def from_behind(value, axis, steps):
    count = lax.axis_size(axis)
    initial, last = (max(0, -steps), min(count, count - steps))
    return lax.ppermute(value, axis, [(source, source + steps) for source in range(initial, last)])


def rope_tables(first, count, head_size):
    half = head_size // 2
    freq = ROPE_BASE ** (-(jnp.arange(half, dtype=jnp.float32) * 2.0 / head_size))
    places = first + jnp.arange(count, dtype=jnp.int32)
    angle = places.astype(jnp.float32)[:, None] * freq[None, :]
    return (jnp.cos(angle)[:, None, :], jnp.sin(angle)[:, None, :])


def apply_rotary(value_rows, cosine_table, sine_table):
    half = value_rows.shape[-1] // 2
    upper = value_rows[..., :half]
    lower = value_rows[..., half:]
    return jnp.concatenate(
        [upper * cosine_table - lower * sine_table, lower * cosine_table + upper * sine_table],
        axis=-1,
    )


def inverse_rotary(value_rows, cosine_table, sine_table):
    half = value_rows.shape[-1] // 2
    upper = value_rows[..., :half]
    lower = value_rows[..., half:]
    return jnp.concatenate(
        [upper * cosine_table + lower * sine_table, lower * cosine_table - upper * sine_table],
        axis=-1,
    )


def sum_over_heads(partial):
    count = lax.axis_size("head")
    me = lax.axis_index("head")
    rows, width = partial.shape
    blocks = partial.reshape(rows, count, width // count)
    total = lax.dynamic_index_in_dim(blocks, me, axis=1, keepdims=False).astype(jnp.float32)
    for shift in range(1, count):
        outgoing = lax.dynamic_index_in_dim(blocks, (me + shift) % count, axis=1, keepdims=False)
        incoming = lax.ppermute(
            outgoing, "head", [(source, (source + shift) % count) for source in range(count)]
        )
        total = total + incoming.astype(jnp.float32)
    return total.astype(jnp.bfloat16)


def row_major(value):
    return with_layout_constraint(value, Layout(tuple(range(value.ndim))))

def dot_rows(left, weight):
    return lax.dot_general(
        left, weight, (((1,), (1,)), ((), ())), preferred_element_type=jnp.float32
    )


def attend_forward(query_rows, key_rows, value_rows, allowed):
    score = jnp.einsum("ngrd,mgd->grnm", query_rows, key_rows, preferred_element_type=jnp.float32)
    score = jnp.where(allowed[None, None], score, NEG_LARGE)
    top = jnp.max(score, axis=-1, keepdims=True)
    expo = jnp.exp(score - top)
    prob = expo / jnp.sum(expo, axis=-1, keepdims=True)
    prob_b = prob.astype(jnp.bfloat16)
    attended = jnp.einsum(
        "grnm,mgd->ngrd", prob_b, value_rows, preferred_element_type=jnp.float32
    ).astype(jnp.bfloat16)
    return (prob, prob_b, attended)


def attend_backward(prob, prob_b, attended, gradient_list, query_rows, key_rows, value_rows, block):
    delta = jnp.sum(gradient_list.astype(jnp.float32) * attended.astype(jnp.float32), axis=-1)
    delta = jnp.transpose(delta, (1, 2, 0))[..., None]
    grad_prob = jnp.einsum(
        "ngrd,mgd->grnm", gradient_list, value_rows, preferred_element_type=jnp.float32
    )
    grad_score = (prob * (grad_prob - delta)).astype(jnp.bfloat16)
    grad_q = jnp.einsum("grnm,mgd->ngrd", grad_score, key_rows, preferred_element_type=jnp.float32)
    grad_k = []
    grad_v = []
    for lowest in range(0, key_rows.shape[0], block):
        grad_k.append(
            jnp.einsum(
                "grnm,ngrd->mgd",
                grad_score[..., lowest : lowest + block],
                query_rows,
                preferred_element_type=jnp.float32,
            )
        )
        grad_v.append(
            jnp.einsum(
                "grnm,ngrd->mgd",
                prob_b[..., lowest : lowest + block],
                gradient_list,
                preferred_element_type=jnp.float32,
            )
        )
    return (grad_q, grad_k, grad_v)


def shards(hidden_in, out_grad, w_query, key_weight, value_weight, w_out):
    rows = hidden_in.shape[0]
    head_size = HEAD_WIDTH
    query_cols = w_query.shape[1]
    key_value_columns = key_weight.shape[1]
    local_heads = query_cols // head_size
    local_groups = key_value_columns // head_size
    group_ratio = local_heads // local_groups
    reach = WINDOW // rows
    first = lax.axis_index("ctx") * rows
    full_qkv = lax.all_gather(
        jnp.concatenate([w_query, key_weight, value_weight], axis=1), "ctx", axis=0, tiled=True
    )
    full_out = lax.all_gather(w_out, "ctx", axis=0, tiled=True)
    projected = jnp.dot(hidden_in, full_qkv, preferred_element_type=jnp.float32)
    query = projected[:, :query_cols]
    key_projected = projected[:, query_cols : query_cols + key_value_columns]
    value_projected = projected[:, query_cols + key_value_columns :]
    cosine_table, sine_table = rope_tables(first, rows, head_size)
    query_rows = (
        apply_rotary(query.reshape(rows, local_heads, head_size), cosine_table, sine_table)
        * QUERY_SCALE
    ).astype(jnp.bfloat16)
    keys_here = (
        apply_rotary(key_projected.reshape(rows, local_groups, head_size), cosine_table, sine_table)
        .astype(jnp.bfloat16)
        .reshape(rows, key_value_columns)
    )
    values_here = value_projected.astype(jnp.bfloat16)
    key_blocks = []
    value_blocks = []
    for distance in range(reach, 0, -1):
        far_keys, far_values = from_behind((keys_here, values_here), "ctx", distance)
        key_blocks.append(far_keys)
        value_blocks.append(far_values)
    keys_all = jnp.concatenate(key_blocks + [keys_here], axis=0).reshape(
        -1, local_groups, head_size
    )
    values_all = jnp.concatenate(value_blocks + [values_here], axis=0).reshape(
        -1, local_groups, head_size
    )
    query_pos = first + jnp.arange(rows, dtype=jnp.int32)
    key_pos = first - reach * rows + jnp.arange((reach + 1) * rows, dtype=jnp.int32)
    allowed = (
        (key_pos[None, :] <= query_pos[:, None])
        & (key_pos[None, :] > query_pos[:, None] - WINDOW)
        & (key_pos[None, :] >= 0)
    )
    grouped_queries = query_rows.reshape(rows, local_groups, group_ratio, head_size)
    prob, prob_b, attended = attend_forward(grouped_queries, keys_all, values_all, allowed)
    attended, late_out_grad = lax.optimization_barrier((attended, out_grad))
    attention_gradient = jnp.dot(
        late_out_grad, full_out, preferred_element_type=jnp.float32
    ).astype(jnp.bfloat16)
    grouped_grads = attention_gradient.reshape(rows, local_groups, group_ratio, head_size)
    attended_flat = attended.reshape(rows, query_cols)
    grad_w_out = jnp.einsum(
        "nd,nc->dc", out_grad, attended_flat, preferred_element_type=jnp.float32
    )
    grad_q, grad_k, grad_v = attend_backward(
        prob, prob_b, attended, grouped_grads, grouped_queries, keys_all, values_all, rows
    )
    grad_k = [part.reshape(rows, key_value_columns) for part in grad_k]
    grad_v = [part.reshape(rows, key_value_columns) for part in grad_v]
    own_keys = grad_k[reach]
    own_values = grad_v[reach]
    for distance in range(1, reach + 1):
        back_keys, back_values = from_behind(
            (
                grad_k[reach - distance].astype(jnp.bfloat16),
                grad_v[reach - distance].astype(jnp.bfloat16),
            ),
            "ctx",
            -distance,
        )
        own_keys = own_keys + back_keys.astype(jnp.float32)
        own_values = own_values + back_values.astype(jnp.float32)
    dquery = (
        (
            inverse_rotary(grad_q.reshape(rows, local_heads, head_size), cosine_table, sine_table)
            * QUERY_SCALE
        )
        .astype(jnp.bfloat16)
        .reshape(rows, query_cols)
    )
    key_gradient = (
        inverse_rotary(own_keys.reshape(rows, local_groups, head_size), cosine_table, sine_table)
        .astype(jnp.bfloat16)
        .reshape(rows, key_value_columns)
    )
    value_gradient = own_values.astype(jnp.bfloat16)
    grads_qkv = jnp.concatenate([dquery, key_gradient, value_gradient], axis=1)
    partial_in = dot_rows(dquery, full_qkv[:, :query_cols]) + dot_rows(
        grads_qkv[:, query_cols:], full_qkv[:, query_cols:]
    )
    in_grad = sum_over_heads(partial_in.astype(jnp.bfloat16))
    grad_qkv_part = jnp.einsum("nd,nc->dc", hidden_in, grads_qkv, preferred_element_type=jnp.float32)
    grad_out_w = lax.psum_scatter(
        row_major(grad_w_out.astype(jnp.bfloat16)), "ctx", scatter_dimension=0, tiled=True
    ).astype(jnp.float32)
    grad_qkv = lax.psum_scatter(
        row_major(grad_qkv_part.astype(jnp.bfloat16)), "ctx", scatter_dimension=0, tiled=True
    ).astype(jnp.float32)
    grad_query = grad_qkv[:, :query_cols]
    grad_key = grad_qkv[:, query_cols : query_cols + key_value_columns]
    grad_value = grad_qkv[:, query_cols + key_value_columns :]
    return (in_grad, grad_query, grad_key, grad_value, grad_out_w)


def solution(mesh):
    in_specs = (
        P("ctx", None),
        P("ctx", None),
        P("ctx", "head"),
        P("ctx", "head"),
        P("ctx", "head"),
        P("ctx", "head"),
    )
    out_specs = (
        P("ctx", "head"),
        P("ctx", "head"),
        P("ctx", "head"),
        P("ctx", "head"),
        P("ctx", "head"),
    )
    return jax.shard_map(shards, mesh=mesh, in_specs=in_specs, out_specs=out_specs, check_vma=False)
```
